512 devices in a mesh: gx: 32 (over y, x), ga: 16 (over z, core).
Axes of the slice: x: 4, y: 8, z: 8, core: 2. Of those that a mesh axis runs over, the one named last changes fastest.
Arguments:
- velocity: float32 [3, 128, 384, 768], P(None, 'gx', 'ga'), may hold values from -6 to 6
- accumulated: float32 [3, 128, 384, 768], P(None, 'gx', 'ga'), may hold values from -6 to 6
- wall_first: float32 [384, 384], replicated, may hold values from -0.3125 to 0.3125
- wall_second: float32 [384, 384], replicated, may hold values from -0.3125 to 0.3125
- recycle_rows: int32 [384], replicated, may hold values from 0 to 382
- weight_index: int32 [384], replicated, may hold values from 0 to 63
- weight_table: float32 [64], replicated, may hold values from 0 to 1
Outputs:
- velocity_next: float32 [3, 128, 384, 768], P(None, 'gx', 'ga')
- accumulated_next: float32 [3, 128, 384, 768], P(None, 'gx', 'ga')
The draws below stay inside these ranges and needn't reach their ends.
Inputs may be any that keep to these rules, and one draw needn't show every extreme that they name: `recycle_rows`: each entry names the lower of two adjacent recycle-plane rows. `weight_index`: each entry names one entry of weight_table.
All inputs are finite; a program needn't handle non-finite values.
Results may differ from the reference program's by a relative error of at most 0.0001.
Values sent between devices are 32-bit elements; how exact they have to be, the bound alone decides.
No kernel may reach another device: no remote copies, remote signals or barrier semaphores. Data moves between devices by JAX's collectives and lax.ppermute only.
A program may use at most 64 MiB of HBM per device.

```python
import math
import jax
import jax.numpy as jnp
from jax import lax

NY = 384
NZ = 768
CX = 4
HALO = 4
NW = 64
NX = 128
RECYCLE_SLAB = 31


def place_ends(entries, own_key, least, largest):
    place = [jax.random.randint(jax.random.fold_in(own_key, axis), (), 0, length) for axis, length in enumerate(entries.shape)]
    widest = entries.shape.index(max(entries.shape))
    next_to = place[:widest] + [(place[widest] + 1) % entries.shape[widest]] + place[widest + 1:]
    return entries.at[tuple(place)].set(least).at[tuple(next_to)].set(largest)


def steps_of(stream_key, shape, split, least, largest):
    def one(position, parts):
        heights = jax.random.uniform(jax.random.fold_in(jax.random.fold_in(stream_key, 6), position), (parts,), jnp.float32, least / len(split), largest / len(split))
        return jnp.repeat(jnp.exp(heights), shape[position] // parts).reshape((-1,) + (1,) * (len(shape) - position - 1))

    factor_of = one(*split[0])
    for cut in split[1:]:
        factor_of = factor_of * one(*cut)
    return factor_of


def bell_draw(key, shape, deviation, most, pieces=(), held_as=jnp.bfloat16):
    result = deviation * jax.random.normal(key, shape, jnp.float32)
    if pieces:
        result = result * steps_of(key, shape, pieces, -0.22, 0.18)
    return jnp.clip(result, -most, most).astype(held_as)


def setup_inputs(seed: int = 0) -> dict:
    seeds = jax.random.split(jax.random.key(seed), 8)
    return {
        "velocity": bell_draw(seeds[0], (3, NX, NY, NZ), 1.0, 6.0, ((1, 32), (2, 16)), jnp.float32),
        "accumulated": bell_draw(seeds[1], (3, NX, NY, NZ), 1.0, 6.0, ((1, 32), (2, 16)), jnp.float32),
        "wall_first": bell_draw(seeds[2], (NY, NY), NY ** -0.5, 0.3125, (), jnp.float32),
        "wall_second": bell_draw(seeds[3], (NY, NY), NY ** -0.5, 0.3125, (), jnp.float32),
        "recycle_rows": place_ends(jax.random.randint(seeds[4], (NY,), 0, NY - 1), jax.random.fold_in(seeds[4], 1), 0, (NY - 1) - 1).astype(jnp.int32),
        "weight_index": place_ends(jax.random.randint(seeds[5], (NY,), 0, NW), jax.random.fold_in(seeds[5], 1), 0, NW - 1).astype(jnp.int32),
        "weight_table": jnp.clip(jax.random.uniform(seeds[6], (NW,), jnp.float32, 0.0, 1.0), 0.0, 1.0),
    }


first_coef = (0.8, -0.2, 4.0 / 105.0, -1.0 / 280.0)
second_coef = (1.6, -0.2, 8.0 / 315.0, -1.0 / 560.0)
center_coef = -205.0 / 72.0
step_size = 0.2
viscosity = 0.2
keep_rate = -5.0 / 9.0
update_rate = 15.0 / 16.0


def streamwise(field, inflow):
    lower = jnp.broadcast_to(inflow[None], (HALO, NY, NZ))
    upper = jnp.broadcast_to(field[-1:], (HALO, NY, NZ))
    padded = jnp.concatenate([lower, field, upper], 0)
    first = jnp.zeros_like(field)
    second = center_coef * field
    for offset in range(1, HALO + 1):
        ahead = padded[HALO + offset:HALO + offset + NX]
        behind = padded[HALO - offset:HALO - offset + NX]
        first = first + first_coef[offset - 1] * (ahead - behind)
        second = second + second_coef[offset - 1] * (ahead + behind)
    return first, second


def spanwise(field):
    spectrum = jnp.fft.rfft(field, axis=-1)
    levels = jnp.arange(NZ // 2 + 1)
    waves = 2.0 * math.pi * levels / NZ
    odd_waves = jnp.where(levels == NZ // 2, 0.0, waves)
    first = jnp.fft.irfft(1j * odd_waves * spectrum, n=NZ, axis=-1)
    second = jnp.fft.irfft(-(waves * waves) * spectrum, n=NZ, axis=-1)
    return first.astype(field.dtype), second.astype(field.dtype)


def reference(velocity, accumulated, wall_first, wall_second, recycle_rows, weight_index, weight_table):
    recycle = velocity[:, RECYCLE_SLAB * CX]
    frac = weight_table[weight_index][None, :, None]
    inflow = (1.0 - frac) * recycle[:, recycle_rows] + frac * recycle[:, recycle_rows + 1]
    outputs_new = []
    outputs_acc = []
    for component in range(3):
        field = velocity[component]
        stream_first, stream_second = streamwise(field, inflow[component])
        normal_first = jnp.einsum('ij,xjz->xiz', wall_first, field, precision=lax.Precision.HIGHEST)
        normal_second = jnp.einsum('ij,xjz->xiz', wall_second, field, precision=lax.Precision.HIGHEST)
        span_first, span_second = spanwise(field)
        tendency = -(velocity[0] * stream_first + velocity[1] * normal_first + velocity[2] * span_first) + viscosity * (stream_second + normal_second + span_second)
        acc_next = keep_rate * accumulated[component] + step_size * tendency
        outputs_acc.append(acc_next)
        outputs_new.append(field + update_rate * acc_next)
    return jnp.stack(outputs_new), jnp.stack(outputs_acc)
```

```python
import math

import numpy as np
import jax
import jax.numpy as jnp
from jax import lax
from jax.sharding import PartitionSpec as P

HALO = 4
RECYCLE_PLANE = 124


first_coef = (0.8, -0.2, 4.0 / 105.0, -1.0 / 280.0)
second_coef = (1.6, -0.2, 8.0 / 315.0, -1.0 / 560.0)
center_coef = -205.0 / 72.0
step_size = 0.2
viscosity = 0.2
keep_rate = -5.0 / 9.0
update_rate = 15.0 / 16.0
HIGHEST = lax.Precision.HIGHEST


def spanwise_table(length):
    places = np.arange(length)
    apart = places[None, :] - places[:, None]
    apart = np.remainder(apart + length // 2, length) - length // 2
    parity = 1.0 - 2.0 * np.remainder(apart, 2)
    spacing = 2.0 * math.pi / length
    angle = apart * (0.5 * spacing)
    same = apart == 0
    safe_sine = np.where(same, 1.0, np.sin(angle))
    first = np.where(same, 0.0, 0.5 * spacing * parity * np.cos(angle) / safe_sine)
    second = np.where(
        same,
        -math.pi * math.pi / 3.0 - spacing * spacing / 6.0,
        -0.5 * spacing * spacing * parity / (safe_sine * safe_sine),
    )
    return np.concatenate([first, second], 1).astype(np.float32)


def ghost_weights(planes):
    lower = [sum(first_coef[m - 1] for m in range(x + 1, HALO + 1)) for x in range(planes)]
    upper = [sum(second_coef[m - 1] for m in range(x + 1, HALO + 1)) for x in range(planes)]
    return np.asarray(lower, np.float32), np.asarray(upper, np.float32)


def streamwise(field):
    count = lax.axis_size("gx")
    extent = field.shape[1]
    behind = lax.ppermute(field, "gx", [(i, i + 1) for i in range(count - 1)])
    ahead = lax.ppermute(field, "gx", [(i + 1, i) for i in range(count - 1)])
    at_outlet = lax.axis_index("gx") == count - 1
    ahead = jnp.where(at_outlet, jnp.broadcast_to(field[:, -1:], ahead.shape), ahead)
    padded = jnp.concatenate([behind[:, extent - HALO :], field, ahead[:, :HALO]], 1)
    first = jnp.zeros_like(field)
    second = center_coef * field
    for offset in range(1, HALO + 1):
        up = padded[:, HALO + offset : HALO + offset + extent]
        down = padded[:, HALO - offset : HALO - offset + extent]
        first = first + first_coef[offset - 1] * (up - down)
        second = second + second_coef[offset - 1] * (up + down)
    return -(field[0:1] * first) + viscosity * second


def interpolation_matrix(recycle_rows, weight_index, weight_table, rows):
    levels = jnp.arange(weight_table.shape[0], dtype=jnp.int32)
    frac = jnp.sum(
        jnp.where(weight_index[:, None] == levels[None, :], weight_table[None, :], 0.0), axis=1
    )[:, None]
    places = jnp.arange(rows, dtype=jnp.int32)[None, :]
    lower = jnp.where(places == recycle_rows[:, None], 1.0 - frac, 0.0)
    upper = jnp.where(places == recycle_rows[:, None] + 1, frac, 0.0)
    return lower + upper


def shards(
    velocity, accumulated, wall_first, wall_second, recycle_rows, weight_index, weight_table
):
    comps, planes, rows_here, span = velocity.shape
    parts = lax.axis_size("ga")
    slabs = lax.axis_size("gx")
    share = span // parts
    rows = rows_here * parts
    width = comps * planes * share

    send = velocity.reshape(comps, planes, rows_here, parts, share)
    send = send.transpose(3, 2, 0, 1, 4).reshape(parts, rows_here, width)
    cols = lax.all_to_all(send, "ga", 0, 0, tiled=True).reshape(rows, width)
    grid = cols.reshape(rows, comps, planes, share)

    source_slab, source_plane = divmod(RECYCLE_PLANE, planes)
    mix = interpolation_matrix(recycle_rows, weight_index, weight_table, rows)
    plane = grid[:, :, source_plane, :].reshape(rows, comps * share)
    inflow = jnp.dot(mix, plane, precision=HIGHEST, preferred_element_type=jnp.float32)
    inflow = lax.ppermute(inflow, "gx", [(source_slab, 0)]).reshape(rows, comps, 1, share)

    both = jnp.concatenate([wall_first, wall_second], 0)
    derived = jnp.dot(both, cols, precision=HIGHEST, preferred_element_type=jnp.float32)
    normal_first = derived[:rows].reshape(rows, comps, planes, share)
    normal_second = derived[rows:].reshape(rows, comps, planes, share)
    wall = -(grid[:, 1:2] * normal_first) + viscosity * normal_second

    lower, upper = ghost_weights(planes)
    ghost = inflow * (grid[:, 0:1] * lower[None, None, :, None] + viscosity * upper[None, None, :, None])
    wall = wall + jnp.where(lax.axis_index("gx") == 0, ghost, 0.0)

    back = lax.all_to_all(wall.reshape(parts, rows_here, width), "ga", 0, 0, tiled=True)
    back = back.reshape(parts, rows_here, comps, planes, share).transpose(2, 3, 1, 0, 4)
    back = back.reshape(comps, planes, rows_here, span)

    lines = velocity.reshape(-1, span)
    spectral = jnp.dot(
        lines,
        jnp.asarray(spanwise_table(span)),
        precision=HIGHEST,
        preferred_element_type=jnp.float32,
    )
    span_first = spectral[:, :span].reshape(velocity.shape)
    span_second = spectral[:, span:].reshape(velocity.shape)

    tendency = -(velocity[2:3] * span_first) + viscosity * span_second
    tendency = tendency + streamwise(velocity)
    tendency = tendency + back
    accumulated_next = keep_rate * accumulated + step_size * tendency
    return (velocity + update_rate * accumulated_next, accumulated_next)


def solution(mesh):
    in_specs = (P(None, "gx", "ga", None), P(None, "gx", "ga", None), P(), P(), P(), P(), P())
    out_specs = (P(None, "gx", "ga", None), P(None, "gx", "ga", None))
    return jax.shard_map(shards, mesh=mesh, in_specs=in_specs, out_specs=out_specs, check_vma=False)
```

```python
import math

import numpy as np
import jax
import jax.numpy as jnp
from jax import lax
from jax.sharding import PartitionSpec as P

HALO = 4
RECYCLE_PLANE = 124


first_coef = (0.8, -0.2, 4.0 / 105.0, -1.0 / 280.0)
second_coef = (1.6, -0.2, 8.0 / 315.0, -1.0 / 560.0)
center_coef = -205.0 / 72.0
step_size = 0.2
viscosity = 0.2
keep_rate = -5.0 / 9.0
update_rate = 15.0 / 16.0
HIGHEST = lax.Precision.HIGHEST


def spanwise_table(length):
    places = np.arange(length)
    apart = places[None, :] - places[:, None]
    apart = np.remainder(apart + length // 2, length) - length // 2
    parity = 1.0 - 2.0 * np.remainder(apart, 2)
    spacing = 2.0 * math.pi / length
    angle = apart * (0.5 * spacing)
    same = apart == 0
    safe_sine = np.where(same, 1.0, np.sin(angle))
    first = np.where(same, 0.0, 0.5 * spacing * parity * np.cos(angle) / safe_sine)
    second = np.where(
        same,
        -math.pi * math.pi / 3.0 - spacing * spacing / 6.0,
        -0.5 * spacing * spacing * parity / (safe_sine * safe_sine),
    )
    return np.concatenate([first, second], 1).astype(np.float32)


def ghost_weights(planes):
    lower = [sum(first_coef[m - 1] for m in range(x + 1, HALO + 1)) for x in range(planes)]
    upper = [sum(second_coef[m - 1] for m in range(x + 1, HALO + 1)) for x in range(planes)]
    return np.asarray(lower, np.float32), np.asarray(upper, np.float32)


def halo_planes(field):
    count = lax.axis_size("gx")
    behind = lax.ppermute(field, "gx", [(i, i + 1) for i in range(count - 1)])
    ahead = lax.ppermute(field, "gx", [(i + 1, i) for i in range(count - 1)])
    return behind, ahead


def streamwise(field, behind, ahead):
    count = lax.axis_size("gx")
    extent = field.shape[1]
    at_outlet = lax.axis_index("gx") == count - 1
    ahead = jnp.where(at_outlet, jnp.broadcast_to(field[:, -1:], ahead.shape), ahead)
    padded = jnp.concatenate([behind[:, extent - HALO :], field, ahead[:, :HALO]], 1)
    first = jnp.zeros_like(field)
    second = center_coef * field
    for offset in range(1, HALO + 1):
        up = padded[:, HALO + offset : HALO + offset + extent]
        down = padded[:, HALO - offset : HALO - offset + extent]
        first = first + first_coef[offset - 1] * (up - down)
        second = second + second_coef[offset - 1] * (up + down)
    return -(field[0:1] * first) + viscosity * second


def interpolation_matrix(recycle_rows, weight_index, weight_table, rows):
    levels = jnp.arange(weight_table.shape[0], dtype=jnp.int32)
    frac = jnp.sum(
        jnp.where(weight_index[:, None] == levels[None, :], weight_table[None, :], 0.0), axis=1
    )[:, None]
    places = jnp.arange(rows, dtype=jnp.int32)[None, :]
    lower = jnp.where(places == recycle_rows[:, None], 1.0 - frac, 0.0)
    upper = jnp.where(places == recycle_rows[:, None] + 1, frac, 0.0)
    return lower + upper


def columns_of(field, parts):
    planes, rows_here, span = field.shape
    share = span // parts
    send = field.reshape(planes, rows_here, parts, share).transpose(2, 1, 0, 3)
    send = send.reshape(parts, rows_here, planes * share)
    return lax.all_to_all(send, "ga", 0, 0, tiled=True).reshape(rows_here * parts, planes * share)


def rows_of(block, parts, planes):
    rows, width = block.shape
    share = width // planes
    back = lax.all_to_all(block.reshape(parts, rows // parts, width), "ga", 0, 0, tiled=True)
    back = back.reshape(parts, rows // parts, planes, share).transpose(2, 1, 0, 3)
    return back.reshape(planes, rows // parts, parts * share)


def shards(
    velocity, accumulated, wall_first, wall_second, recycle_rows, weight_index, weight_table
):
    comps, planes, rows_here, span = velocity.shape
    parts = lax.axis_size("ga")
    share = span // parts
    rows = rows_here * parts
    contract_rows = (((0,), (1,)), ((), ()))
    contract_lead = (((0,), (0,)), ((), ()))

    behind, ahead = halo_planes(velocity)
    cols = [columns_of(velocity[c], parts) for c in range(comps)]

    lines = velocity.reshape(-1, span)
    spectral = jnp.dot(
        lines,
        jnp.asarray(spanwise_table(span)),
        precision=HIGHEST,
        preferred_element_type=jnp.float32,
    )
    span_first = spectral[:, :span].reshape(velocity.shape)
    span_second = spectral[:, span:].reshape(velocity.shape)
    span_terms = -(velocity[2:3] * span_first) + viscosity * span_second
    cols, span_terms, behind, ahead = lax.optimization_barrier((cols, span_terms, behind, ahead))

    source_slab, source_plane = divmod(RECYCLE_PLANE, planes)
    mix = interpolation_matrix(recycle_rows, weight_index, weight_table, rows)
    inflow = jnp.concatenate(
        [
            lax.dot_general(
                cols[c][:, source_plane * share : (source_plane + 1) * share],
                mix,
                contract_rows,
                precision=HIGHEST,
                preferred_element_type=jnp.float32,
            )
            for c in range(comps)
        ],
        0,
    )
    inflow = lax.ppermute(inflow, "gx", [(source_slab, 0)])

    lower, upper = ghost_weights(planes)
    lower = jnp.asarray(np.repeat(lower, share))
    upper = jnp.asarray(np.repeat(upper, share))
    spread = jnp.asarray(np.tile(np.eye(share, dtype=np.float32), (1, planes)))
    at_inlet = lax.axis_index("gx") == 0
    both = jnp.concatenate([wall_first, wall_second], 0)
    backs = []
    for c in range(comps):
        derived = jnp.dot(both, cols[c], precision=HIGHEST, preferred_element_type=jnp.float32)
        wall = -(cols[1] * derived[:rows]) + viscosity * derived[rows:]
        spread_inflow = lax.dot_general(
            inflow[c * share : (c + 1) * share],
            spread,
            contract_lead,
            precision=HIGHEST,
            preferred_element_type=jnp.float32,
        )
        ghost = spread_inflow * (cols[0] * lower + viscosity * upper)
        wall = wall + jnp.where(at_inlet, ghost, 0.0)
        backs.append(rows_of(wall, parts, planes))
    back = jnp.stack(backs)

    tendency = span_terms + streamwise(velocity, behind, ahead)
    tendency = tendency + back
    accumulated_next = keep_rate * accumulated + step_size * tendency
    return (velocity + update_rate * accumulated_next, accumulated_next)


def solution(mesh):
    in_specs = (P(None, "gx", "ga", None), P(None, "gx", "ga", None), P(), P(), P(), P(), P())
    out_specs = (P(None, "gx", "ga", None), P(None, "gx", "ga", None))
    return jax.shard_map(shards, mesh=mesh, in_specs=in_specs, out_specs=out_specs, check_vma=False)
```

```python
import math

import numpy as np
import jax
import jax.numpy as jnp
from jax import lax
from jax.sharding import PartitionSpec as P

HALO = 4
RECYCLE_PLANE = 124


first_coef = (0.8, -0.2, 4.0 / 105.0, -1.0 / 280.0)
second_coef = (1.6, -0.2, 8.0 / 315.0, -1.0 / 560.0)
center_coef = -205.0 / 72.0
step_size = 0.2
viscosity = 0.2
keep_rate = -5.0 / 9.0
update_rate = 15.0 / 16.0
HIGHEST = lax.Precision.HIGHEST


def spanwise_table(length):
    places = np.arange(length)
    apart = places[None, :] - places[:, None]
    apart = np.remainder(apart + length // 2, length) - length // 2
    parity = 1.0 - 2.0 * np.remainder(apart, 2)
    spacing = 2.0 * math.pi / length
    angle = apart * (0.5 * spacing)
    same = apart == 0
    safe_sine = np.where(same, 1.0, np.sin(angle))
    first = np.where(same, 0.0, 0.5 * spacing * parity * np.cos(angle) / safe_sine)
    second = np.where(
        same,
        -math.pi * math.pi / 3.0 - spacing * spacing / 6.0,
        -0.5 * spacing * spacing * parity / (safe_sine * safe_sine),
    )
    return np.concatenate([first, second], 1).astype(np.float32)


def ghost_weights(planes):
    lower = [sum(first_coef[m - 1] for m in range(x + 1, HALO + 1)) for x in range(planes)]
    upper = [sum(second_coef[m - 1] for m in range(x + 1, HALO + 1)) for x in range(planes)]
    return np.asarray(lower, np.float32), np.asarray(upper, np.float32)


def halo_planes(field):
    count = lax.axis_size("gx")
    behind = lax.ppermute(field, "gx", [(i, i + 1) for i in range(count - 1)])
    ahead = lax.ppermute(field, "gx", [(i + 1, i) for i in range(count - 1)])
    return behind, ahead


def streamwise(field, behind, ahead):
    count = lax.axis_size("gx")
    extent = field.shape[1]
    at_outlet = lax.axis_index("gx") == count - 1
    ahead = jnp.where(at_outlet, jnp.broadcast_to(field[:, -1:], ahead.shape), ahead)
    padded = jnp.concatenate([behind[:, extent - HALO :], field, ahead[:, :HALO]], 1)
    first = jnp.zeros_like(field)
    second = center_coef * field
    for offset in range(1, HALO + 1):
        up = padded[:, HALO + offset : HALO + offset + extent]
        down = padded[:, HALO - offset : HALO - offset + extent]
        first = first + first_coef[offset - 1] * (up - down)
        second = second + second_coef[offset - 1] * (up + down)
    return -(field[0:1] * first) + viscosity * second


def interpolation_matrix(recycle_rows, weight_index, weight_table, rows):
    levels = jnp.arange(weight_table.shape[0], dtype=jnp.int32)
    frac = jnp.sum(
        jnp.where(weight_index[:, None] == levels[None, :], weight_table[None, :], 0.0), axis=1
    )[:, None]
    places = jnp.arange(rows, dtype=jnp.int32)[None, :]
    lower = jnp.where(places == recycle_rows[:, None], 1.0 - frac, 0.0)
    upper = jnp.where(places == recycle_rows[:, None] + 1, frac, 0.0)
    return lower + upper


def shards(
    velocity, accumulated, wall_first, wall_second, recycle_rows, weight_index, weight_table
):
    comps, planes, rows_here, span = velocity.shape
    parts = lax.axis_size("ga")
    slabs = lax.axis_size("gx")
    share = span // parts
    rows = rows_here * parts
    width = comps * planes * share

    send = velocity.reshape(comps, planes, rows_here, parts, share)
    send = send.transpose(3, 2, 0, 1, 4).reshape(parts, rows_here, width)
    behind, ahead = halo_planes(velocity)
    cols = lax.all_to_all(send, "ga", 0, 0, tiled=True).reshape(rows, width)
    lines = velocity.reshape(-1, span)
    spectral = jnp.dot(
        lines,
        jnp.asarray(spanwise_table(span)),
        precision=HIGHEST,
        preferred_element_type=jnp.float32,
    )
    span_first = spectral[:, :span].reshape(velocity.shape)
    span_second = spectral[:, span:].reshape(velocity.shape)

    span_terms = -(velocity[2:3] * span_first) + viscosity * span_second
    cols, span_terms, behind, ahead = lax.optimization_barrier((cols, span_terms, behind, ahead))
    grid = cols.reshape(rows, comps, planes, share)

    source_slab, source_plane = divmod(RECYCLE_PLANE, planes)
    mix = interpolation_matrix(recycle_rows, weight_index, weight_table, rows)
    plane = grid[:, :, source_plane, :].reshape(rows, comps * share)
    inflow = jnp.dot(mix, plane, precision=HIGHEST, preferred_element_type=jnp.float32)
    inflow = lax.ppermute(inflow, "gx", [(source_slab, 0)]).reshape(rows, comps, 1, share)

    both = jnp.concatenate([wall_first, wall_second], 0)
    derived = jnp.dot(both, cols, precision=HIGHEST, preferred_element_type=jnp.float32)
    normal_first = derived[:rows].reshape(rows, comps, planes, share)
    normal_second = derived[rows:].reshape(rows, comps, planes, share)
    wall = -(grid[:, 1:2] * normal_first) + viscosity * normal_second

    lower, upper = ghost_weights(planes)
    ghost = inflow * (grid[:, 0:1] * lower[None, None, :, None] + viscosity * upper[None, None, :, None])
    wall = wall + jnp.where(lax.axis_index("gx") == 0, ghost, 0.0)

    back = lax.all_to_all(wall.reshape(parts, rows_here, width), "ga", 0, 0, tiled=True)
    back = back.reshape(parts, rows_here, comps, planes, share).transpose(2, 3, 1, 0, 4)
    back = back.reshape(comps, planes, rows_here, span)

    tendency = span_terms + streamwise(velocity, behind, ahead)
    tendency = tendency + back
    accumulated_next = keep_rate * accumulated + step_size * tendency
    return (velocity + update_rate * accumulated_next, accumulated_next)


def solution(mesh):
    in_specs = (P(None, "gx", "ga", None), P(None, "gx", "ga", None), P(), P(), P(), P(), P())
    out_specs = (P(None, "gx", "ga", None), P(None, "gx", "ga", None))
    return jax.shard_map(shards, mesh=mesh, in_specs=in_specs, out_specs=out_specs, check_vma=False)
```

```python
import math

import numpy as np
import jax
import jax.numpy as jnp
from jax import lax
from jax.experimental import pallas as pl
from jax.experimental.pallas import tpu as pltpu
from jax.sharding import PartitionSpec as P

HALO = 4
RECYCLE_PLANE = 124


first_coef = (0.8, -0.2, 4.0 / 105.0, -1.0 / 280.0)
second_coef = (1.6, -0.2, 8.0 / 315.0, -1.0 / 560.0)
center_coef = -205.0 / 72.0
step_size = 0.2
viscosity = 0.2
keep_rate = -5.0 / 9.0
update_rate = 15.0 / 16.0
HIGHEST = lax.Precision.HIGHEST


def spanwise_table(length):
    places = np.arange(length)
    apart = places[None, :] - places[:, None]
    apart = np.remainder(apart + length // 2, length) - length // 2
    parity = 1.0 - 2.0 * np.remainder(apart, 2)
    spacing = 2.0 * math.pi / length
    angle = apart * (0.5 * spacing)
    same = apart == 0
    safe_sine = np.where(same, 1.0, np.sin(angle))
    first = np.where(same, 0.0, 0.5 * spacing * parity * np.cos(angle) / safe_sine)
    second = np.where(
        same,
        -math.pi * math.pi / 3.0 - spacing * spacing / 6.0,
        -0.5 * spacing * spacing * parity / (safe_sine * safe_sine),
    )
    return np.concatenate([first, second], 1).astype(np.float32)


def ghost_weights(planes):
    lower = [sum(first_coef[m - 1] for m in range(x + 1, HALO + 1)) for x in range(planes)]
    upper = [sum(second_coef[m - 1] for m in range(x + 1, HALO + 1)) for x in range(planes)]
    return np.asarray(lower, np.float32), np.asarray(upper, np.float32)


def halo_planes(field):
    count = lax.axis_size("gx")
    behind = lax.ppermute(field, "gx", [(i, i + 1) for i in range(count - 1)])
    ahead = lax.ppermute(field, "gx", [(i + 1, i) for i in range(count - 1)])
    return behind, ahead


def streamwise(field, behind, ahead):
    count = lax.axis_size("gx")
    extent = field.shape[1]
    at_outlet = lax.axis_index("gx") == count - 1
    ahead = jnp.where(at_outlet, jnp.broadcast_to(field[:, -1:], ahead.shape), ahead)
    padded = jnp.concatenate([behind[:, extent - HALO :], field, ahead[:, :HALO]], 1)
    first = jnp.zeros_like(field)
    second = center_coef * field
    for offset in range(1, HALO + 1):
        up = padded[:, HALO + offset : HALO + offset + extent]
        down = padded[:, HALO - offset : HALO - offset + extent]
        first = first + first_coef[offset - 1] * (up - down)
        second = second + second_coef[offset - 1] * (up + down)
    return -(field[0:1] * first) + viscosity * second


def interpolation_matrix(recycle_rows, weight_index, weight_table, rows):
    levels = jnp.arange(weight_table.shape[0], dtype=jnp.int32)
    frac = jnp.sum(
        jnp.where(weight_index[:, None] == levels[None, :], weight_table[None, :], 0.0), axis=1
    )[:, None]
    places = jnp.arange(rows, dtype=jnp.int32)[None, :]
    lower = jnp.where(places == recycle_rows[:, None], 1.0 - frac, 0.0)
    upper = jnp.where(places == recycle_rows[:, None] + 1, frac, 0.0)
    return lower + upper


def pack_columns(velocity, parts):
    comps, planes, rows_here, span = velocity.shape
    share = span // parts

    def kernel(v_ref, o_ref):
        for d in range(parts):
            pieces = [
                v_ref[c, x, :, share * d : share * (d + 1)] for c in range(comps) for x in range(planes)
            ]
            o_ref[d] = jnp.concatenate(pieces, axis=1)

    return pl.pallas_call(
        kernel,
        out_shape=jax.ShapeDtypeStruct((parts, rows_here, comps * planes * share), jnp.float32),
    )(velocity)


def wall_block(cols, both, inflow, inlet, planes):
    rows, width = cols.shape
    comps = 3
    share = width // (comps * planes)
    lower, upper = ghost_weights(planes)

    def kernel(inlet_ref, c_ref, w_ref, f_ref, o_ref):
        derived = jnp.dot(w_ref[...], c_ref[...], precision=HIGHEST, preferred_element_type=jnp.float32)
        block = planes * share
        v1 = c_ref[:, block : 2 * block]
        at_inlet = inlet_ref[0] > 0
        for c in range(comps):
            first = derived[:rows, c * block : (c + 1) * block]
            second = derived[rows:, c * block : (c + 1) * block]
            wall = -(v1 * first) + viscosity * second
            flow = f_ref[:, c * share : (c + 1) * share]
            ghost = jnp.concatenate(
                [
                    flow * (c_ref[:, x * share : (x + 1) * share] * lower[x] + viscosity * upper[x])
                    for x in range(planes)
                ],
                axis=1,
            )
            o_ref[:, c * block : (c + 1) * block] = wall + jnp.where(at_inlet, ghost, 0.0)

    return pl.pallas_call(
        kernel,
        out_shape=jax.ShapeDtypeStruct((rows, width), jnp.float32),
        in_specs=[
            pl.BlockSpec(memory_space=pltpu.SMEM),
            pl.BlockSpec(memory_space=pltpu.VMEM),
            pl.BlockSpec(memory_space=pltpu.VMEM),
            pl.BlockSpec(memory_space=pltpu.VMEM),
        ],
    )(inlet, cols, both, inflow)


def combine(velocity, accumulated, local_terms, back):
    comps, planes, rows_here, span = velocity.shape
    parts = back.shape[0]
    share = span // parts

    def kernel(v_ref, a_ref, t_ref, b_ref, nv_ref, na_ref):
        for c in range(comps):
            for x in range(planes):
                k = (c * planes + x) * share
                wall = jnp.concatenate([b_ref[d, :, k : k + share] for d in range(parts)], axis=1)
                tendency = t_ref[c, x] + wall
                acc = keep_rate * a_ref[c, x] + step_size * tendency
                na_ref[c, x] = acc
                nv_ref[c, x] = v_ref[c, x] + update_rate * acc

    shape = jax.ShapeDtypeStruct(velocity.shape, jnp.float32)
    return pl.pallas_call(kernel, out_shape=(shape, shape))(velocity, accumulated, local_terms, back)


def shards(
    velocity, accumulated, wall_first, wall_second, recycle_rows, weight_index, weight_table
):
    comps, planes, rows_here, span = velocity.shape
    parts = lax.axis_size("ga")
    share = span // parts
    rows = rows_here * parts
    width = comps * planes * share

    behind, ahead = halo_planes(velocity)
    send = pack_columns(velocity, parts)
    cols = lax.all_to_all(send, "ga", 0, 0, tiled=True).reshape(rows, width)
    lines = velocity.reshape(-1, span)
    spectral = jnp.dot(
        lines,
        jnp.asarray(spanwise_table(span)),
        precision=HIGHEST,
        preferred_element_type=jnp.float32,
    )
    span_first = spectral[:, :span].reshape(velocity.shape)
    span_second = spectral[:, span:].reshape(velocity.shape)
    span_terms = -(velocity[2:3] * span_first) + viscosity * span_second
    cols, span_terms, behind, ahead = lax.optimization_barrier((cols, span_terms, behind, ahead))

    source_slab, source_plane = divmod(RECYCLE_PLANE, planes)
    mix = interpolation_matrix(recycle_rows, weight_index, weight_table, rows)
    plane = jnp.concatenate(
        [cols[:, (c * planes + source_plane) * share : (c * planes + source_plane + 1) * share] for c in range(comps)],
        axis=1,
    )
    inflow = jnp.dot(mix, plane, precision=HIGHEST, preferred_element_type=jnp.float32)
    inflow = lax.ppermute(inflow, "gx", [(source_slab, 0)])

    both = jnp.concatenate([wall_first, wall_second], 0)
    inlet = (lax.axis_index("gx") == 0).astype(jnp.int32).reshape(1)
    wall = wall_block(cols, both, inflow, inlet, planes)
    back = lax.all_to_all(wall.reshape(parts, rows_here, width), "ga", 0, 0, tiled=True)

    local_terms = span_terms + streamwise(velocity, behind, ahead)
    return combine(velocity, accumulated, local_terms, back)


def solution(mesh):
    in_specs = (P(None, "gx", "ga", None), P(None, "gx", "ga", None), P(), P(), P(), P(), P())
    out_specs = (P(None, "gx", "ga", None), P(None, "gx", "ga", None))
    return jax.shard_map(shards, mesh=mesh, in_specs=in_specs, out_specs=out_specs, check_vma=False)
```

```python
import math

import numpy as np
import jax
import jax.numpy as jnp
from jax import lax
from jax.experimental import pallas as pl
from jax.experimental.pallas import tpu as pltpu
from jax.sharding import PartitionSpec as P

HALO = 4
RECYCLE_PLANE = 124


first_coef = (0.8, -0.2, 4.0 / 105.0, -1.0 / 280.0)
second_coef = (1.6, -0.2, 8.0 / 315.0, -1.0 / 560.0)
center_coef = -205.0 / 72.0
step_size = 0.2
viscosity = 0.2
keep_rate = -5.0 / 9.0
update_rate = 15.0 / 16.0
HIGHEST = lax.Precision.HIGHEST


def spanwise_table(length):
    places = np.arange(length)
    apart = places[None, :] - places[:, None]
    apart = np.remainder(apart + length // 2, length) - length // 2
    parity = 1.0 - 2.0 * np.remainder(apart, 2)
    spacing = 2.0 * math.pi / length
    angle = apart * (0.5 * spacing)
    same = apart == 0
    safe_sine = np.where(same, 1.0, np.sin(angle))
    first = np.where(same, 0.0, 0.5 * spacing * parity * np.cos(angle) / safe_sine)
    second = np.where(
        same,
        -math.pi * math.pi / 3.0 - spacing * spacing / 6.0,
        -0.5 * spacing * spacing * parity / (safe_sine * safe_sine),
    )
    return np.concatenate([first, second], 1).astype(np.float32)


def ghost_weights(planes):
    lower = [sum(first_coef[m - 1] for m in range(x + 1, HALO + 1)) for x in range(planes)]
    upper = [sum(second_coef[m - 1] for m in range(x + 1, HALO + 1)) for x in range(planes)]
    return np.asarray(lower, np.float32), np.asarray(upper, np.float32)


def halo_planes(field):
    count = lax.axis_size("gx")
    behind = lax.ppermute(field, "gx", [(i, i + 1) for i in range(count - 1)])
    ahead = lax.ppermute(field, "gx", [(i + 1, i) for i in range(count - 1)])
    return behind, ahead


def streamwise(field, behind, ahead):
    count = lax.axis_size("gx")
    extent = field.shape[1]
    at_outlet = lax.axis_index("gx") == count - 1
    ahead = jnp.where(at_outlet, jnp.broadcast_to(field[:, -1:], ahead.shape), ahead)
    padded = jnp.concatenate([behind[:, extent - HALO :], field, ahead[:, :HALO]], 1)
    first = jnp.zeros_like(field)
    second = center_coef * field
    for offset in range(1, HALO + 1):
        up = padded[:, HALO + offset : HALO + offset + extent]
        down = padded[:, HALO - offset : HALO - offset + extent]
        first = first + first_coef[offset - 1] * (up - down)
        second = second + second_coef[offset - 1] * (up + down)
    return -(field[0:1] * first) + viscosity * second


def interpolation_matrix(recycle_rows, weight_index, weight_table, rows):
    levels = jnp.arange(weight_table.shape[0], dtype=jnp.int32)
    frac = jnp.sum(
        jnp.where(weight_index[:, None] == levels[None, :], weight_table[None, :], 0.0), axis=1
    )[:, None]
    places = jnp.arange(rows, dtype=jnp.int32)[None, :]
    lower = jnp.where(places == recycle_rows[:, None], 1.0 - frac, 0.0)
    upper = jnp.where(places == recycle_rows[:, None] + 1, frac, 0.0)
    return lower + upper


def pack_columns(velocity, parts):
    comps, planes, rows_here, span = velocity.shape
    share = span // parts

    def kernel(v_ref, o_ref):
        for d in range(parts):
            pieces = [
                v_ref[c, x, :, share * d : share * (d + 1)] for c in range(comps) for x in range(planes)
            ]
            o_ref[d] = jnp.concatenate(pieces, axis=1)

    return pl.pallas_call(
        kernel,
        out_shape=jax.ShapeDtypeStruct((parts, rows_here, comps * planes * share), jnp.float32),
    )(velocity)


def wall_block(cols, wall_first, wall_second, planes):
    rows, width = cols.shape
    comps = 3
    block = width // comps

    def kernel(c_ref, f_ref, s_ref, o_ref):
        field = c_ref[...]
        first = jnp.dot(f_ref[...], field, precision=HIGHEST, preferred_element_type=jnp.float32)
        second = jnp.dot(s_ref[...], field, precision=HIGHEST, preferred_element_type=jnp.float32)
        v1 = c_ref[:, block : 2 * block]
        for c in range(comps):
            part = slice(c * block, (c + 1) * block)
            o_ref[:, part] = -(v1 * first[:, part]) + viscosity * second[:, part]

    return pl.pallas_call(kernel, out_shape=jax.ShapeDtypeStruct((rows, width), jnp.float32))(
        cols, wall_first, wall_second
    )


def add_ghost(wall, cols, inflow, inlet, planes):
    rows, width = cols.shape
    comps = 3
    share = width // (comps * planes)
    block = planes * share
    lower, upper = ghost_weights(planes)

    def kernel(inlet_ref, w_ref, c_ref, f_ref, o_ref):
        at_inlet = inlet_ref[0] > 0
        for c in range(comps):
            flow = f_ref[:, c * share : (c + 1) * share]
            ghost = jnp.concatenate(
                [
                    flow * (c_ref[:, x * share : (x + 1) * share] * lower[x] + viscosity * upper[x])
                    for x in range(planes)
                ],
                axis=1,
            )
            part = slice(c * block, (c + 1) * block)
            o_ref[:, part] = w_ref[:, part] + jnp.where(at_inlet, ghost, 0.0)

    return pl.pallas_call(
        kernel,
        out_shape=jax.ShapeDtypeStruct((rows, width), jnp.float32),
        in_specs=[
            pl.BlockSpec(memory_space=pltpu.SMEM),
            pl.BlockSpec(memory_space=pltpu.VMEM),
            pl.BlockSpec(memory_space=pltpu.VMEM),
            pl.BlockSpec(memory_space=pltpu.VMEM),
        ],
        input_output_aliases={1: 0},
    )(inlet, wall, cols, inflow)


def combine(velocity, accumulated, local_terms, back):
    comps, planes, rows_here, span = velocity.shape
    parts = back.shape[0]
    share = span // parts

    def kernel(v_ref, a_ref, t_ref, b_ref, nv_ref, na_ref):
        for c in range(comps):
            for x in range(planes):
                k = (c * planes + x) * share
                wall = jnp.concatenate([b_ref[d, :, k : k + share] for d in range(parts)], axis=1)
                tendency = t_ref[c, x] + wall
                acc = keep_rate * a_ref[c, x] + step_size * tendency
                na_ref[c, x] = acc
                nv_ref[c, x] = v_ref[c, x] + update_rate * acc

    shape = jax.ShapeDtypeStruct(velocity.shape, jnp.float32)
    return pl.pallas_call(kernel, out_shape=(shape, shape))(velocity, accumulated, local_terms, back)


def shards(
    velocity, accumulated, wall_first, wall_second, recycle_rows, weight_index, weight_table
):
    comps, planes, rows_here, span = velocity.shape
    parts = lax.axis_size("ga")
    share = span // parts
    rows = rows_here * parts
    width = comps * planes * share

    behind, ahead = halo_planes(velocity)
    send = pack_columns(velocity, parts)
    cols = lax.all_to_all(send, "ga", 0, 0, tiled=True).reshape(rows, width)
    cols, behind, ahead, field = lax.optimization_barrier((cols, behind, ahead, velocity))

    source_slab, source_plane = divmod(RECYCLE_PLANE, planes)
    mix = interpolation_matrix(recycle_rows, weight_index, weight_table, rows)
    plane = jnp.concatenate(
        [cols[:, (c * planes + source_plane) * share : (c * planes + source_plane + 1) * share] for c in range(comps)],
        axis=1,
    )
    inflow = jnp.dot(mix, plane, precision=HIGHEST, preferred_element_type=jnp.float32)
    inflow = lax.ppermute(inflow, "gx", [(source_slab, 0)])

    wall = wall_block(cols, wall_first, wall_second, planes)
    lines = field.reshape(-1, span)
    spectral = jnp.dot(
        lines,
        jnp.asarray(spanwise_table(span)),
        precision=HIGHEST,
        preferred_element_type=jnp.float32,
    )
    span_first = spectral[:, :span].reshape(velocity.shape)
    span_second = spectral[:, span:].reshape(velocity.shape)
    span_terms = -(field[2:3] * span_first) + viscosity * span_second
    inflow, wall, span_terms = lax.optimization_barrier((inflow, wall, span_terms))

    inlet = (lax.axis_index("gx") == 0).astype(jnp.int32).reshape(1)
    wall = add_ghost(wall, cols, inflow, inlet, planes)
    back = lax.all_to_all(wall.reshape(parts, rows_here, width), "ga", 0, 0, tiled=True)

    local_terms = span_terms + streamwise(velocity, behind, ahead)
    return combine(velocity, accumulated, local_terms, back)


def solution(mesh):
    in_specs = (P(None, "gx", "ga", None), P(None, "gx", "ga", None), P(), P(), P(), P(), P())
    out_specs = (P(None, "gx", "ga", None), P(None, "gx", "ga", None))
    return jax.shard_map(shards, mesh=mesh, in_specs=in_specs, out_specs=out_specs, check_vma=False)
```

```python
import math

import numpy as np
import jax
import jax.numpy as jnp
from jax import lax
from jax.experimental import pallas as pl
from jax.experimental.pallas import tpu as pltpu
from jax.sharding import PartitionSpec as P

HALO = 4
RECYCLE_PLANE = 124


first_coef = (0.8, -0.2, 4.0 / 105.0, -1.0 / 280.0)
second_coef = (1.6, -0.2, 8.0 / 315.0, -1.0 / 560.0)
center_coef = -205.0 / 72.0
step_size = 0.2
viscosity = 0.2
keep_rate = -5.0 / 9.0
update_rate = 15.0 / 16.0
HIGHEST = lax.Precision.HIGHEST


def spanwise_table(length):
    places = np.arange(length)
    apart = places[None, :] - places[:, None]
    apart = np.remainder(apart + length // 2, length) - length // 2
    parity = 1.0 - 2.0 * np.remainder(apart, 2)
    spacing = 2.0 * math.pi / length
    angle = apart * (0.5 * spacing)
    same = apart == 0
    safe_sine = np.where(same, 1.0, np.sin(angle))
    first = np.where(same, 0.0, 0.5 * spacing * parity * np.cos(angle) / safe_sine)
    second = np.where(
        same,
        -math.pi * math.pi / 3.0 - spacing * spacing / 6.0,
        -0.5 * spacing * spacing * parity / (safe_sine * safe_sine),
    )
    return np.concatenate([first, second], 1).astype(np.float32)


def ghost_weights(planes):
    lower = [sum(first_coef[m - 1] for m in range(x + 1, HALO + 1)) for x in range(planes)]
    upper = [sum(second_coef[m - 1] for m in range(x + 1, HALO + 1)) for x in range(planes)]
    return np.asarray(lower, np.float32), np.asarray(upper, np.float32)


def halo_planes(field):
    count = lax.axis_size("gx")
    behind = lax.ppermute(field, "gx", [(i, i + 1) for i in range(count - 1)])
    ahead = lax.ppermute(field, "gx", [(i + 1, i) for i in range(count - 1)])
    return behind, ahead


def streamwise(field, behind, ahead):
    count = lax.axis_size("gx")
    extent = field.shape[1]
    at_outlet = lax.axis_index("gx") == count - 1
    ahead = jnp.where(at_outlet, jnp.broadcast_to(field[:, -1:], ahead.shape), ahead)
    padded = jnp.concatenate([behind[:, extent - HALO :], field, ahead[:, :HALO]], 1)
    first = jnp.zeros_like(field)
    second = center_coef * field
    for offset in range(1, HALO + 1):
        up = padded[:, HALO + offset : HALO + offset + extent]
        down = padded[:, HALO - offset : HALO - offset + extent]
        first = first + first_coef[offset - 1] * (up - down)
        second = second + second_coef[offset - 1] * (up + down)
    return -(field[0:1] * first) + viscosity * second


def interpolation_matrix(recycle_rows, weight_index, weight_table, rows):
    levels = jnp.arange(weight_table.shape[0], dtype=jnp.int32)
    frac = jnp.sum(
        jnp.where(weight_index[:, None] == levels[None, :], weight_table[None, :], 0.0), axis=1
    )[:, None]
    places = jnp.arange(rows, dtype=jnp.int32)[None, :]
    lower = jnp.where(places == recycle_rows[:, None], 1.0 - frac, 0.0)
    upper = jnp.where(places == recycle_rows[:, None] + 1, frac, 0.0)
    return lower + upper


def pack_columns(velocity, parts):
    comps, planes, rows_here, span = velocity.shape
    share = span // parts

    def kernel(v_ref, o_ref):
        for d in range(parts):
            pieces = [
                v_ref[c, x, :, share * d : share * (d + 1)] for c in range(comps) for x in range(planes)
            ]
            o_ref[d] = jnp.concatenate(pieces, axis=1)

    return pl.pallas_call(
        kernel,
        out_shape=jax.ShapeDtypeStruct((parts, rows_here, comps * planes * share), jnp.float32),
    )(velocity)


def wall_block(cols, wall_first, wall_second, planes):
    rows, width = cols.shape
    comps = 3
    block = width // comps

    def kernel(c_ref, f_ref, s_ref, o_ref):
        field = c_ref[...]
        first = jnp.dot(f_ref[...], field, precision=HIGHEST, preferred_element_type=jnp.float32)
        second = jnp.dot(s_ref[...], field, precision=HIGHEST, preferred_element_type=jnp.float32)
        v1 = c_ref[:, block : 2 * block]
        for c in range(comps):
            part = slice(c * block, (c + 1) * block)
            o_ref[:, part] = -(v1 * first[:, part]) + viscosity * second[:, part]

    return pl.pallas_call(kernel, out_shape=jax.ShapeDtypeStruct((rows, width), jnp.float32))(
        cols, wall_first, wall_second
    )


def add_ghost(wall, cols, inflow, inlet, planes):
    rows, width = cols.shape
    comps = 3
    share = width // (comps * planes)
    block = planes * share
    lower, upper = ghost_weights(planes)

    def kernel(inlet_ref, w_ref, c_ref, f_ref, o_ref):
        at_inlet = inlet_ref[0] > 0
        for c in range(comps):
            flow = f_ref[:, c * share : (c + 1) * share]
            ghost = jnp.concatenate(
                [
                    flow * (c_ref[:, x * share : (x + 1) * share] * lower[x] + viscosity * upper[x])
                    for x in range(planes)
                ],
                axis=1,
            )
            part = slice(c * block, (c + 1) * block)
            o_ref[:, part] = w_ref[:, part] + jnp.where(at_inlet, ghost, 0.0)

    return pl.pallas_call(
        kernel,
        out_shape=jax.ShapeDtypeStruct((rows, width), jnp.float32),
        in_specs=[
            pl.BlockSpec(memory_space=pltpu.SMEM),
            pl.BlockSpec(memory_space=pltpu.VMEM),
            pl.BlockSpec(memory_space=pltpu.VMEM),
            pl.BlockSpec(memory_space=pltpu.VMEM),
        ],
        input_output_aliases={1: 0},
    )(inlet, wall, cols, inflow)


def combine(velocity, accumulated, local_terms, back):
    comps, planes, rows_here, span = velocity.shape
    parts = back.shape[0]
    share = span // parts

    def kernel(v_ref, a_ref, t_ref, b_ref, nv_ref, na_ref):
        for c in range(comps):
            for x in range(planes):
                k = (c * planes + x) * share
                wall = jnp.concatenate([b_ref[d, :, k : k + share] for d in range(parts)], axis=1)
                tendency = t_ref[c, x] + wall
                acc = keep_rate * a_ref[c, x] + step_size * tendency
                na_ref[c, x] = acc
                nv_ref[c, x] = v_ref[c, x] + update_rate * acc

    shape = jax.ShapeDtypeStruct(velocity.shape, jnp.float32)
    return pl.pallas_call(kernel, out_shape=(shape, shape))(velocity, accumulated, local_terms, back)


def shards(
    velocity, accumulated, wall_first, wall_second, recycle_rows, weight_index, weight_table
):
    comps, planes, rows_here, span = velocity.shape
    parts = lax.axis_size("ga")
    share = span // parts
    rows = rows_here * parts
    width = comps * planes * share

    behind, ahead = halo_planes(velocity)
    send = pack_columns(velocity, parts)
    cols = lax.all_to_all(send, "ga", 0, 0, tiled=True).reshape(rows, width)
    lines = velocity.reshape(-1, span)
    spectral = jnp.dot(
        lines,
        jnp.asarray(spanwise_table(span)),
        precision=HIGHEST,
        preferred_element_type=jnp.float32,
    )
    span_first = spectral[:, :span].reshape(velocity.shape)
    span_second = spectral[:, span:].reshape(velocity.shape)
    span_terms = -(velocity[2:3] * span_first) + viscosity * span_second
    cols, behind, ahead, span_terms = lax.optimization_barrier((cols, behind, ahead, span_terms))

    source_slab, source_plane = divmod(RECYCLE_PLANE, planes)
    mix = interpolation_matrix(recycle_rows, weight_index, weight_table, rows)
    plane = jnp.concatenate(
        [cols[:, (c * planes + source_plane) * share : (c * planes + source_plane + 1) * share] for c in range(comps)],
        axis=1,
    )
    inflow = jnp.dot(mix, plane, precision=HIGHEST, preferred_element_type=jnp.float32)
    inflow = lax.ppermute(inflow, "gx", [(source_slab, 0)])

    wall = wall_block(cols, wall_first, wall_second, planes)
    inflow, wall = lax.optimization_barrier((inflow, wall))

    inlet = (lax.axis_index("gx") == 0).astype(jnp.int32).reshape(1)
    wall = add_ghost(wall, cols, inflow, inlet, planes)
    back = lax.all_to_all(wall.reshape(parts, rows_here, width), "ga", 0, 0, tiled=True)

    local_terms = span_terms + streamwise(velocity, behind, ahead)
    return combine(velocity, accumulated, local_terms, back)


def solution(mesh):
    in_specs = (P(None, "gx", "ga", None), P(None, "gx", "ga", None), P(), P(), P(), P(), P())
    out_specs = (P(None, "gx", "ga", None), P(None, "gx", "ga", None))
    return jax.shard_map(shards, mesh=mesh, in_specs=in_specs, out_specs=out_specs, check_vma=False)
```

```python
import math

import numpy as np
import jax
import jax.numpy as jnp
from jax import lax
from jax.experimental import pallas as pl
from jax.experimental.pallas import tpu as pltpu
from jax.sharding import PartitionSpec as P

HALO = 4
RECYCLE_PLANE = 124


first_coef = (0.8, -0.2, 4.0 / 105.0, -1.0 / 280.0)
second_coef = (1.6, -0.2, 8.0 / 315.0, -1.0 / 560.0)
center_coef = -205.0 / 72.0
step_size = 0.2
viscosity = 0.2
keep_rate = -5.0 / 9.0
update_rate = 15.0 / 16.0
HIGHEST = lax.Precision.HIGHEST


def spanwise_table(length):
    places = np.arange(length)
    apart = places[None, :] - places[:, None]
    apart = np.remainder(apart + length // 2, length) - length // 2
    parity = 1.0 - 2.0 * np.remainder(apart, 2)
    spacing = 2.0 * math.pi / length
    angle = apart * (0.5 * spacing)
    same = apart == 0
    safe_sine = np.where(same, 1.0, np.sin(angle))
    first = np.where(same, 0.0, 0.5 * spacing * parity * np.cos(angle) / safe_sine)
    second = np.where(
        same,
        -math.pi * math.pi / 3.0 - spacing * spacing / 6.0,
        -0.5 * spacing * spacing * parity / (safe_sine * safe_sine),
    )
    return np.concatenate([first, second], 1).astype(np.float32)


def ghost_weights(planes):
    lower = [sum(first_coef[m - 1] for m in range(x + 1, HALO + 1)) for x in range(planes)]
    upper = [sum(second_coef[m - 1] for m in range(x + 1, HALO + 1)) for x in range(planes)]
    return np.asarray(lower, np.float32), np.asarray(upper, np.float32)


def halo_planes(field):
    count = lax.axis_size("gx")
    behind = lax.ppermute(field, "gx", [(i, i + 1) for i in range(count - 1)])
    ahead = lax.ppermute(field, "gx", [(i + 1, i) for i in range(count - 1)])
    return behind, ahead


def streamwise(field, behind, ahead):
    count = lax.axis_size("gx")
    extent = field.shape[1]
    at_outlet = lax.axis_index("gx") == count - 1
    ahead = jnp.where(at_outlet, jnp.broadcast_to(field[:, -1:], ahead.shape), ahead)
    padded = jnp.concatenate([behind[:, extent - HALO :], field, ahead[:, :HALO]], 1)
    first = jnp.zeros_like(field)
    second = center_coef * field
    for offset in range(1, HALO + 1):
        up = padded[:, HALO + offset : HALO + offset + extent]
        down = padded[:, HALO - offset : HALO - offset + extent]
        first = first + first_coef[offset - 1] * (up - down)
        second = second + second_coef[offset - 1] * (up + down)
    return -(field[0:1] * first) + viscosity * second


def interpolation_matrix(recycle_rows, weight_index, weight_table, rows):
    levels = jnp.arange(weight_table.shape[0], dtype=jnp.int32)
    frac = jnp.sum(
        jnp.where(weight_index[:, None] == levels[None, :], weight_table[None, :], 0.0), axis=1
    )[:, None]
    places = jnp.arange(rows, dtype=jnp.int32)[None, :]
    lower = jnp.where(places == recycle_rows[:, None], 1.0 - frac, 0.0)
    upper = jnp.where(places == recycle_rows[:, None] + 1, frac, 0.0)
    return lower + upper


def pack_columns(velocity, parts):
    comps, planes, rows_here, span = velocity.shape
    share = span // parts

    def kernel(v_ref, o_ref):
        for d in range(parts):
            pieces = [
                v_ref[c, x, :, share * d : share * (d + 1)] for c in range(comps) for x in range(planes)
            ]
            o_ref[d] = jnp.concatenate(pieces, axis=1)

    return pl.pallas_call(
        kernel,
        out_shape=jax.ShapeDtypeStruct((parts, rows_here, comps * planes * share), jnp.float32),
    )(velocity)


def wall_block(cols, wall_first, wall_second, planes):
    rows, width = cols.shape
    comps = 3
    block = width // comps

    def kernel(c_ref, f_ref, s_ref, o_ref):
        field = c_ref[...]
        first = jnp.dot(f_ref[...], field, precision=HIGHEST, preferred_element_type=jnp.float32)
        second = jnp.dot(s_ref[...], field, precision=HIGHEST, preferred_element_type=jnp.float32)
        v1 = c_ref[:, block : 2 * block]
        for c in range(comps):
            part = slice(c * block, (c + 1) * block)
            o_ref[:, part] = -(v1 * first[:, part]) + viscosity * second[:, part]

    return pl.pallas_call(kernel, out_shape=jax.ShapeDtypeStruct((rows, width), jnp.float32))(
        cols, wall_first, wall_second
    )


def combine(velocity, accumulated, local_terms, back, inflow, inlet):
    comps, planes, rows_here, span = velocity.shape
    parts = back.shape[0]
    share = span // parts
    lower, upper = ghost_weights(planes)

    def kernel(inlet_ref, v_ref, a_ref, t_ref, b_ref, f_ref, nv_ref, na_ref):
        at_inlet = inlet_ref[0] > 0
        for c in range(comps):
            flow = jnp.concatenate(
                [f_ref[d, :, c * share : (c + 1) * share] for d in range(parts)], axis=1
            )
            for x in range(planes):
                k = (c * planes + x) * share
                wall = jnp.concatenate([b_ref[d, :, k : k + share] for d in range(parts)], axis=1)
                ghost = flow * (v_ref[0, x] * lower[x] + viscosity * upper[x])
                tendency = t_ref[c, x] + wall + jnp.where(at_inlet, ghost, 0.0)
                acc = keep_rate * a_ref[c, x] + step_size * tendency
                na_ref[c, x] = acc
                nv_ref[c, x] = v_ref[c, x] + update_rate * acc

    shape = jax.ShapeDtypeStruct(velocity.shape, jnp.float32)
    vmem = pl.BlockSpec(memory_space=pltpu.VMEM)
    return pl.pallas_call(
        kernel,
        out_shape=(shape, shape),
        in_specs=[pl.BlockSpec(memory_space=pltpu.SMEM)] + [vmem] * 5,
    )(inlet, velocity, accumulated, local_terms, back, inflow)


def shards(
    velocity, accumulated, wall_first, wall_second, recycle_rows, weight_index, weight_table
):
    comps, planes, rows_here, span = velocity.shape
    parts = lax.axis_size("ga")
    share = span // parts
    rows = rows_here * parts
    width = comps * planes * share

    behind, ahead = halo_planes(velocity)
    send = pack_columns(velocity, parts)
    cols = lax.all_to_all(send, "ga", 0, 0, tiled=True).reshape(rows, width)
    lines = velocity.reshape(-1, span)
    spectral = jnp.dot(
        lines,
        jnp.asarray(spanwise_table(span)),
        precision=HIGHEST,
        preferred_element_type=jnp.float32,
    )
    span_first = spectral[:, :span].reshape(velocity.shape)
    span_second = spectral[:, span:].reshape(velocity.shape)
    span_terms = -(velocity[2:3] * span_first) + viscosity * span_second
    cols, behind, ahead, span_terms = lax.optimization_barrier((cols, behind, ahead, span_terms))

    source_slab, source_plane = divmod(RECYCLE_PLANE, planes)
    mix = interpolation_matrix(recycle_rows, weight_index, weight_table, rows)
    plane = jnp.concatenate(
        [cols[:, (c * planes + source_plane) * share : (c * planes + source_plane + 1) * share] for c in range(comps)],
        axis=1,
    )
    inflow = jnp.dot(mix, plane, precision=HIGHEST, preferred_element_type=jnp.float32)
    inflow = lax.ppermute(inflow, "gx", [(source_slab, 0)])

    wall = wall_block(cols, wall_first, wall_second, planes)
    back = lax.all_to_all(wall.reshape(parts, rows_here, width), "ga", 0, 0, tiled=True)
    local_terms = span_terms + streamwise(velocity, behind, ahead)
    inflow, back, local_terms = lax.optimization_barrier((inflow, back, local_terms))
    inflow = lax.all_to_all(inflow.reshape(parts, rows_here, comps * share), "ga", 0, 0, tiled=True)

    inlet = (lax.axis_index("gx") == 0).astype(jnp.int32).reshape(1)
    return combine(velocity, accumulated, local_terms, back, inflow, inlet)


def solution(mesh):
    in_specs = (P(None, "gx", "ga", None), P(None, "gx", "ga", None), P(), P(), P(), P(), P())
    out_specs = (P(None, "gx", "ga", None), P(None, "gx", "ga", None))
    return jax.shard_map(shards, mesh=mesh, in_specs=in_specs, out_specs=out_specs, check_vma=False)
```

```python
import math

import numpy as np
import jax
import jax.numpy as jnp
from jax import lax
from jax.experimental import pallas as pl
from jax.experimental.pallas import tpu as pltpu
from jax.sharding import PartitionSpec as P

HALO = 4
RECYCLE_PLANE = 124


first_coef = (0.8, -0.2, 4.0 / 105.0, -1.0 / 280.0)
second_coef = (1.6, -0.2, 8.0 / 315.0, -1.0 / 560.0)
center_coef = -205.0 / 72.0
step_size = 0.2
viscosity = 0.2
keep_rate = -5.0 / 9.0
update_rate = 15.0 / 16.0
HIGHEST = lax.Precision.HIGHEST


def spanwise_table(length):
    places = np.arange(length)
    apart = places[None, :] - places[:, None]
    apart = np.remainder(apart + length // 2, length) - length // 2
    parity = 1.0 - 2.0 * np.remainder(apart, 2)
    spacing = 2.0 * math.pi / length
    angle = apart * (0.5 * spacing)
    same = apart == 0
    safe_sine = np.where(same, 1.0, np.sin(angle))
    first = np.where(same, 0.0, 0.5 * spacing * parity * np.cos(angle) / safe_sine)
    second = np.where(
        same,
        -math.pi * math.pi / 3.0 - spacing * spacing / 6.0,
        -0.5 * spacing * spacing * parity / (safe_sine * safe_sine),
    )
    return np.concatenate([first, second], 1).astype(np.float32)


def ghost_weights(planes):
    lower = [sum(first_coef[m - 1] for m in range(x + 1, HALO + 1)) for x in range(planes)]
    upper = [sum(second_coef[m - 1] for m in range(x + 1, HALO + 1)) for x in range(planes)]
    return np.asarray(lower, np.float32), np.asarray(upper, np.float32)


def halo_planes(field):
    count = lax.axis_size("gx")
    behind = lax.ppermute(field, "gx", [(i, i + 1) for i in range(count - 1)])
    ahead = lax.ppermute(field, "gx", [(i + 1, i) for i in range(count - 1)])
    return behind, ahead


def streamwise(field, behind, ahead):
    count = lax.axis_size("gx")
    extent = field.shape[1]
    at_outlet = lax.axis_index("gx") == count - 1
    ahead = jnp.where(at_outlet, jnp.broadcast_to(field[:, -1:], ahead.shape), ahead)
    padded = jnp.concatenate([behind[:, extent - HALO :], field, ahead[:, :HALO]], 1)
    first = jnp.zeros_like(field)
    second = center_coef * field
    for offset in range(1, HALO + 1):
        up = padded[:, HALO + offset : HALO + offset + extent]
        down = padded[:, HALO - offset : HALO - offset + extent]
        first = first + first_coef[offset - 1] * (up - down)
        second = second + second_coef[offset - 1] * (up + down)
    return -(field[0:1] * first) + viscosity * second


def interpolation_matrix(recycle_rows, weight_index, weight_table, rows):
    levels = jnp.arange(weight_table.shape[0], dtype=jnp.int32)
    frac = jnp.sum(
        jnp.where(weight_index[:, None] == levels[None, :], weight_table[None, :], 0.0), axis=1
    )[:, None]
    places = jnp.arange(rows, dtype=jnp.int32)[None, :]
    lower = jnp.where(places == recycle_rows[:, None], 1.0 - frac, 0.0)
    upper = jnp.where(places == recycle_rows[:, None] + 1, frac, 0.0)
    return lower + upper


def pack_columns(velocity, parts):
    comps, planes, rows_here, span = velocity.shape
    share = span // parts

    def kernel(v_ref, o_ref):
        for d in range(parts):
            pieces = [
                v_ref[c, x, :, share * d : share * (d + 1)] for c in range(comps) for x in range(planes)
            ]
            o_ref[d] = jnp.concatenate(pieces, axis=1)

    return pl.pallas_call(
        kernel,
        out_shape=jax.ShapeDtypeStruct((parts, rows_here, comps * planes * share), jnp.float32),
    )(velocity)


def wall_block(cols, wall_first, wall_second, planes):
    rows, width = cols.shape
    comps = 3
    block = width // comps

    def kernel(c_ref, f_ref, s_ref, o_ref):
        field = c_ref[...]
        first = jnp.dot(f_ref[...], field, precision=HIGHEST, preferred_element_type=jnp.float32)
        second = jnp.dot(s_ref[...], field, precision=HIGHEST, preferred_element_type=jnp.float32)
        v1 = c_ref[:, block : 2 * block]
        for c in range(comps):
            part = slice(c * block, (c + 1) * block)
            o_ref[:, part] = -(v1 * first[:, part]) + viscosity * second[:, part]

    return pl.pallas_call(kernel, out_shape=jax.ShapeDtypeStruct((rows, width), jnp.float32))(
        cols, wall_first, wall_second
    )


def add_ghost(wall, cols, inflow, inlet, planes):
    rows, width = cols.shape
    comps = 3
    share = width // (comps * planes)
    block = planes * share
    lower, upper = ghost_weights(planes)

    def kernel(inlet_ref, w_ref, c_ref, f_ref, o_ref):
        at_inlet = inlet_ref[0] > 0
        for c in range(comps):
            flow = f_ref[:, c * share : (c + 1) * share]
            ghost = jnp.concatenate(
                [
                    flow * (c_ref[:, x * share : (x + 1) * share] * lower[x] + viscosity * upper[x])
                    for x in range(planes)
                ],
                axis=1,
            )
            part = slice(c * block, (c + 1) * block)
            o_ref[:, part] = w_ref[:, part] + jnp.where(at_inlet, ghost, 0.0)

    return pl.pallas_call(
        kernel,
        out_shape=jax.ShapeDtypeStruct((rows, width), jnp.float32),
        in_specs=[
            pl.BlockSpec(memory_space=pltpu.SMEM),
            pl.BlockSpec(memory_space=pltpu.VMEM),
            pl.BlockSpec(memory_space=pltpu.VMEM),
            pl.BlockSpec(memory_space=pltpu.VMEM),
        ],
        input_output_aliases={1: 0},
    )(inlet, wall, cols, inflow)


def combine(velocity, accumulated, local_terms, back):
    comps, planes, rows_here, span = velocity.shape
    parts = back.shape[0]
    share = span // parts

    def kernel(v_ref, a_ref, t_ref, b_ref, nv_ref, na_ref):
        for c in range(comps):
            for x in range(planes):
                k = (c * planes + x) * share
                wall = jnp.concatenate([b_ref[d, :, k : k + share] for d in range(parts)], axis=1)
                tendency = t_ref[c, x] + wall
                acc = keep_rate * a_ref[c, x] + step_size * tendency
                na_ref[c, x] = acc
                nv_ref[c, x] = v_ref[c, x] + update_rate * acc

    shape = jax.ShapeDtypeStruct(velocity.shape, jnp.float32)
    return pl.pallas_call(kernel, out_shape=(shape, shape))(velocity, accumulated, local_terms, back)


def shards(
    velocity, accumulated, wall_first, wall_second, recycle_rows, weight_index, weight_table
):
    comps, planes, rows_here, span = velocity.shape
    parts = lax.axis_size("ga")
    share = span // parts
    rows = rows_here * parts
    width = comps * planes * share

    send = pack_columns(velocity, parts)
    cols = lax.all_to_all(send, "ga", 0, 0, tiled=True).reshape(rows, width)
    lines = velocity.reshape(-1, span)
    spectral = jnp.dot(
        lines,
        jnp.asarray(spanwise_table(span)),
        precision=HIGHEST,
        preferred_element_type=jnp.float32,
    )
    span_first = spectral[:, :span].reshape(velocity.shape)
    span_second = spectral[:, span:].reshape(velocity.shape)
    span_terms = -(velocity[2:3] * span_first) + viscosity * span_second
    span_terms, halo_source = lax.optimization_barrier((span_terms, velocity))
    behind, ahead = halo_planes(halo_source)
    cols, span_terms = lax.optimization_barrier((cols, span_terms))

    source_slab, source_plane = divmod(RECYCLE_PLANE, planes)
    mix = interpolation_matrix(recycle_rows, weight_index, weight_table, rows)
    plane = jnp.concatenate(
        [cols[:, (c * planes + source_plane) * share : (c * planes + source_plane + 1) * share] for c in range(comps)],
        axis=1,
    )
    inflow = jnp.dot(mix, plane, precision=HIGHEST, preferred_element_type=jnp.float32)
    inflow = lax.ppermute(inflow, "gx", [(source_slab, 0)])

    wall = wall_block(cols, wall_first, wall_second, planes)
    inflow, wall = lax.optimization_barrier((inflow, wall))

    inlet = (lax.axis_index("gx") == 0).astype(jnp.int32).reshape(1)
    wall = add_ghost(wall, cols, inflow, inlet, planes)
    back = lax.all_to_all(wall.reshape(parts, rows_here, width), "ga", 0, 0, tiled=True)

    local_terms = span_terms + streamwise(velocity, behind, ahead)
    return combine(velocity, accumulated, local_terms, back)


def solution(mesh):
    in_specs = (P(None, "gx", "ga", None), P(None, "gx", "ga", None), P(), P(), P(), P(), P())
    out_specs = (P(None, "gx", "ga", None), P(None, "gx", "ga", None))
    return jax.shard_map(shards, mesh=mesh, in_specs=in_specs, out_specs=out_specs, check_vma=False)
```

```python
import math

import numpy as np
import jax
import jax.numpy as jnp
from jax import lax
from jax.experimental import pallas as pl
from jax.experimental.pallas import tpu as pltpu
from jax.sharding import PartitionSpec as P

HALO = 4
RECYCLE_PLANE = 124


first_coef = (0.8, -0.2, 4.0 / 105.0, -1.0 / 280.0)
second_coef = (1.6, -0.2, 8.0 / 315.0, -1.0 / 560.0)
center_coef = -205.0 / 72.0
step_size = 0.2
viscosity = 0.2
keep_rate = -5.0 / 9.0
update_rate = 15.0 / 16.0
HIGHEST = lax.Precision.HIGHEST


def spanwise_table(length):
    places = np.arange(length)
    apart = places[None, :] - places[:, None]
    apart = np.remainder(apart + length // 2, length) - length // 2
    parity = 1.0 - 2.0 * np.remainder(apart, 2)
    spacing = 2.0 * math.pi / length
    angle = apart * (0.5 * spacing)
    same = apart == 0
    safe_sine = np.where(same, 1.0, np.sin(angle))
    first = np.where(same, 0.0, 0.5 * spacing * parity * np.cos(angle) / safe_sine)
    second = np.where(
        same,
        -math.pi * math.pi / 3.0 - spacing * spacing / 6.0,
        -0.5 * spacing * spacing * parity / (safe_sine * safe_sine),
    )
    return np.concatenate([first, second], 1).astype(np.float32)


def ghost_weights(planes):
    lower = [sum(first_coef[m - 1] for m in range(x + 1, HALO + 1)) for x in range(planes)]
    upper = [sum(second_coef[m - 1] for m in range(x + 1, HALO + 1)) for x in range(planes)]
    return np.asarray(lower, np.float32), np.asarray(upper, np.float32)


def halo_planes(field):
    count = lax.axis_size("gx")
    behind = lax.ppermute(field, "gx", [(i, i + 1) for i in range(count - 1)])
    ahead = lax.ppermute(field, "gx", [(i + 1, i) for i in range(count - 1)])
    return behind, ahead


def streamwise(field, behind, ahead):
    count = lax.axis_size("gx")
    extent = field.shape[1]
    at_outlet = lax.axis_index("gx") == count - 1
    ahead = jnp.where(at_outlet, jnp.broadcast_to(field[:, -1:], ahead.shape), ahead)
    padded = jnp.concatenate([behind[:, extent - HALO :], field, ahead[:, :HALO]], 1)
    first = jnp.zeros_like(field)
    second = center_coef * field
    for offset in range(1, HALO + 1):
        up = padded[:, HALO + offset : HALO + offset + extent]
        down = padded[:, HALO - offset : HALO - offset + extent]
        first = first + first_coef[offset - 1] * (up - down)
        second = second + second_coef[offset - 1] * (up + down)
    return -(field[0:1] * first) + viscosity * second


def interpolation_matrix(recycle_rows, weight_index, weight_table, rows):
    levels = jnp.arange(weight_table.shape[0], dtype=jnp.int32)
    frac = jnp.sum(
        jnp.where(weight_index[:, None] == levels[None, :], weight_table[None, :], 0.0), axis=1
    )[:, None]
    places = jnp.arange(rows, dtype=jnp.int32)[None, :]
    lower = jnp.where(places == recycle_rows[:, None], 1.0 - frac, 0.0)
    upper = jnp.where(places == recycle_rows[:, None] + 1, frac, 0.0)
    return lower + upper


def pack_columns(velocity, parts):
    comps, planes, rows_here, span = velocity.shape
    share = span // parts

    def kernel(v_ref, o_ref):
        for d in range(parts):
            pieces = [
                v_ref[c, x, :, share * d : share * (d + 1)] for c in range(comps) for x in range(planes)
            ]
            o_ref[d] = jnp.concatenate(pieces, axis=1)

    return pl.pallas_call(
        kernel,
        out_shape=jax.ShapeDtypeStruct((parts, rows_here, comps * planes * share), jnp.float32),
    )(velocity)


def wall_block(cols, wall_first, wall_second, planes):
    rows, width = cols.shape
    comps = 3
    block = width // comps

    def kernel(c_ref, f_ref, s_ref, o_ref):
        field = c_ref[...]
        first = jnp.dot(f_ref[...], field, precision=HIGHEST, preferred_element_type=jnp.float32)
        second = jnp.dot(s_ref[...], field, precision=HIGHEST, preferred_element_type=jnp.float32)
        v1 = c_ref[:, block : 2 * block]
        for c in range(comps):
            part = slice(c * block, (c + 1) * block)
            o_ref[:, part] = -(v1 * first[:, part]) + viscosity * second[:, part]

    return pl.pallas_call(kernel, out_shape=jax.ShapeDtypeStruct((rows, width), jnp.float32))(
        cols, wall_first, wall_second
    )


def add_ghost(wall, cols, inflow, inlet, planes):
    rows, width = cols.shape
    comps = 3
    share = width // (comps * planes)
    block = planes * share
    lower, upper = ghost_weights(planes)

    def kernel(inlet_ref, w_ref, c_ref, f_ref, o_ref):
        at_inlet = inlet_ref[0] > 0
        for c in range(comps):
            flow = f_ref[:, c * share : (c + 1) * share]
            ghost = jnp.concatenate(
                [
                    flow * (c_ref[:, x * share : (x + 1) * share] * lower[x] + viscosity * upper[x])
                    for x in range(planes)
                ],
                axis=1,
            )
            part = slice(c * block, (c + 1) * block)
            o_ref[:, part] = w_ref[:, part] + jnp.where(at_inlet, ghost, 0.0)

    return pl.pallas_call(
        kernel,
        out_shape=jax.ShapeDtypeStruct((rows, width), jnp.float32),
        in_specs=[
            pl.BlockSpec(memory_space=pltpu.SMEM),
            pl.BlockSpec(memory_space=pltpu.VMEM),
            pl.BlockSpec(memory_space=pltpu.VMEM),
            pl.BlockSpec(memory_space=pltpu.VMEM),
        ],
        input_output_aliases={1: 0},
    )(inlet, wall, cols, inflow)


def combine(velocity, accumulated, local_terms, back):
    comps, planes, rows_here, span = velocity.shape
    parts = back.shape[0]
    share = span // parts

    def kernel(v_ref, a_ref, t_ref, b_ref, nv_ref, na_ref):
        for c in range(comps):
            for x in range(planes):
                k = (c * planes + x) * share
                wall = jnp.concatenate([b_ref[d, :, k : k + share] for d in range(parts)], axis=1)
                tendency = t_ref[c, x] + wall
                acc = keep_rate * a_ref[c, x] + step_size * tendency
                na_ref[c, x] = acc
                nv_ref[c, x] = v_ref[c, x] + update_rate * acc

    shape = jax.ShapeDtypeStruct(velocity.shape, jnp.float32)
    return pl.pallas_call(kernel, out_shape=(shape, shape))(velocity, accumulated, local_terms, back)


def shards(
    velocity, accumulated, wall_first, wall_second, recycle_rows, weight_index, weight_table
):
    comps, planes, rows_here, span = velocity.shape
    parts = lax.axis_size("ga")
    share = span // parts
    rows = rows_here * parts
    width = comps * planes * share

    send = pack_columns(velocity, parts)
    cols = lax.all_to_all(send, "ga", 0, 0, tiled=True).reshape(rows, width)
    lines = velocity.reshape(-1, span)
    spectral = jnp.dot(
        lines,
        jnp.asarray(spanwise_table(span)),
        precision=HIGHEST,
        preferred_element_type=jnp.float32,
    )
    span_first = spectral[:, :span].reshape(velocity.shape)
    span_second = spectral[:, span:].reshape(velocity.shape)
    span_terms = -(velocity[2:3] * span_first) + viscosity * span_second
    span_terms, halo_source = lax.optimization_barrier((span_terms, velocity))
    behind, ahead = halo_planes(halo_source)
    cols, span_terms, behind = lax.optimization_barrier((cols, span_terms, behind))

    source_slab, source_plane = divmod(RECYCLE_PLANE, planes)
    mix = interpolation_matrix(recycle_rows, weight_index, weight_table, rows)
    plane = jnp.concatenate(
        [cols[:, (c * planes + source_plane) * share : (c * planes + source_plane + 1) * share] for c in range(comps)],
        axis=1,
    )
    inflow = jnp.dot(mix, plane, precision=HIGHEST, preferred_element_type=jnp.float32)
    inflow = lax.ppermute(inflow, "gx", [(source_slab, 0)])

    wall = wall_block(cols, wall_first, wall_second, planes)
    inflow, wall = lax.optimization_barrier((inflow, wall))

    inlet = (lax.axis_index("gx") == 0).astype(jnp.int32).reshape(1)
    wall = add_ghost(wall, cols, inflow, inlet, planes)
    back = lax.all_to_all(wall.reshape(parts, rows_here, width), "ga", 0, 0, tiled=True)

    local_terms = span_terms + streamwise(velocity, behind, ahead)
    return combine(velocity, accumulated, local_terms, back)


def solution(mesh):
    in_specs = (P(None, "gx", "ga", None), P(None, "gx", "ga", None), P(), P(), P(), P(), P())
    out_specs = (P(None, "gx", "ga", None), P(None, "gx", "ga", None))
    return jax.shard_map(shards, mesh=mesh, in_specs=in_specs, out_specs=out_specs, check_vma=False)
```

```python
import math

import numpy as np
import jax
import jax.numpy as jnp
from jax import lax
from jax.experimental import pallas as pl
from jax.experimental.pallas import tpu as pltpu
from jax.sharding import PartitionSpec as P

HALO = 4
RECYCLE_PLANE = 124


first_coef = (0.8, -0.2, 4.0 / 105.0, -1.0 / 280.0)
second_coef = (1.6, -0.2, 8.0 / 315.0, -1.0 / 560.0)
center_coef = -205.0 / 72.0
step_size = 0.2
viscosity = 0.2
keep_rate = -5.0 / 9.0
update_rate = 15.0 / 16.0
HIGHEST = lax.Precision.HIGHEST


def spanwise_table(length):
    places = np.arange(length)
    apart = places[None, :] - places[:, None]
    apart = np.remainder(apart + length // 2, length) - length // 2
    parity = 1.0 - 2.0 * np.remainder(apart, 2)
    spacing = 2.0 * math.pi / length
    angle = apart * (0.5 * spacing)
    same = apart == 0
    safe_sine = np.where(same, 1.0, np.sin(angle))
    first = np.where(same, 0.0, 0.5 * spacing * parity * np.cos(angle) / safe_sine)
    second = np.where(
        same,
        -math.pi * math.pi / 3.0 - spacing * spacing / 6.0,
        -0.5 * spacing * spacing * parity / (safe_sine * safe_sine),
    )
    return np.concatenate([first, second], 1).astype(np.float32)


def ghost_weights(planes):
    lower = [sum(first_coef[m - 1] for m in range(x + 1, HALO + 1)) for x in range(planes)]
    upper = [sum(second_coef[m - 1] for m in range(x + 1, HALO + 1)) for x in range(planes)]
    return np.asarray(lower, np.float32), np.asarray(upper, np.float32)


def halo_planes(field):
    count = lax.axis_size("gx")
    behind = lax.ppermute(field, "gx", [(i, i + 1) for i in range(count - 1)])
    ahead = lax.ppermute(field, "gx", [(i + 1, i) for i in range(count - 1)])
    return behind, ahead


def streamwise(field, behind, ahead):
    count = lax.axis_size("gx")
    extent = field.shape[1]
    at_outlet = lax.axis_index("gx") == count - 1
    ahead = jnp.where(at_outlet, jnp.broadcast_to(field[:, -1:], ahead.shape), ahead)
    padded = jnp.concatenate([behind[:, extent - HALO :], field, ahead[:, :HALO]], 1)
    first = jnp.zeros_like(field)
    second = center_coef * field
    for offset in range(1, HALO + 1):
        up = padded[:, HALO + offset : HALO + offset + extent]
        down = padded[:, HALO - offset : HALO - offset + extent]
        first = first + first_coef[offset - 1] * (up - down)
        second = second + second_coef[offset - 1] * (up + down)
    return -(field[0:1] * first) + viscosity * second


def interpolation_matrix(recycle_rows, weight_index, weight_table, rows):
    levels = jnp.arange(weight_table.shape[0], dtype=jnp.int32)
    frac = jnp.sum(
        jnp.where(weight_index[:, None] == levels[None, :], weight_table[None, :], 0.0), axis=1
    )[:, None]
    places = jnp.arange(rows, dtype=jnp.int32)[None, :]
    lower = jnp.where(places == recycle_rows[:, None], 1.0 - frac, 0.0)
    upper = jnp.where(places == recycle_rows[:, None] + 1, frac, 0.0)
    return lower + upper


def pack_columns(velocity, parts):
    comps, planes, rows_here, span = velocity.shape
    share = span // parts

    def kernel(v_ref, o_ref):
        for d in range(parts):
            pieces = [
                v_ref[c, x, :, share * d : share * (d + 1)] for c in range(comps) for x in range(planes)
            ]
            o_ref[d] = jnp.concatenate(pieces, axis=1)

    return pl.pallas_call(
        kernel,
        out_shape=jax.ShapeDtypeStruct((parts, rows_here, comps * planes * share), jnp.float32),
    )(velocity)


def wall_block(cols, wall_first, wall_second, planes):
    rows, width = cols.shape
    comps = 3
    block = width // comps

    def kernel(c_ref, f_ref, s_ref, o_ref):
        field = c_ref[...]
        first = jnp.dot(f_ref[...], field, precision=HIGHEST, preferred_element_type=jnp.float32)
        second = jnp.dot(s_ref[...], field, precision=HIGHEST, preferred_element_type=jnp.float32)
        v1 = c_ref[:, block : 2 * block]
        for c in range(comps):
            part = slice(c * block, (c + 1) * block)
            o_ref[:, part] = -(v1 * first[:, part]) + viscosity * second[:, part]

    return pl.pallas_call(kernel, out_shape=jax.ShapeDtypeStruct((rows, width), jnp.float32))(
        cols, wall_first, wall_second
    )


def add_ghost(wall, cols, inflow, inlet, planes):
    rows, width = cols.shape
    comps = 3
    share = width // (comps * planes)
    block = planes * share
    lower, upper = ghost_weights(planes)

    def kernel(inlet_ref, w_ref, c_ref, f_ref, o_ref):
        at_inlet = inlet_ref[0] > 0
        for c in range(comps):
            flow = f_ref[:, c * share : (c + 1) * share]
            ghost = jnp.concatenate(
                [
                    flow * (c_ref[:, x * share : (x + 1) * share] * lower[x] + viscosity * upper[x])
                    for x in range(planes)
                ],
                axis=1,
            )
            part = slice(c * block, (c + 1) * block)
            o_ref[:, part] = w_ref[:, part] + jnp.where(at_inlet, ghost, 0.0)

    return pl.pallas_call(
        kernel,
        out_shape=jax.ShapeDtypeStruct((rows, width), jnp.float32),
        in_specs=[
            pl.BlockSpec(memory_space=pltpu.SMEM),
            pl.BlockSpec(memory_space=pltpu.VMEM),
            pl.BlockSpec(memory_space=pltpu.VMEM),
            pl.BlockSpec(memory_space=pltpu.VMEM),
        ],
        input_output_aliases={1: 0},
    )(inlet, wall, cols, inflow)


def combine(velocity, accumulated, local_terms, back):
    comps, planes, rows_here, span = velocity.shape
    parts = back.shape[0]
    share = span // parts

    def kernel(v_ref, a_ref, t_ref, b_ref, nv_ref, na_ref):
        for c in range(comps):
            for x in range(planes):
                k = (c * planes + x) * share
                wall = jnp.concatenate([b_ref[d, :, k : k + share] for d in range(parts)], axis=1)
                tendency = t_ref[c, x] + wall
                acc = keep_rate * a_ref[c, x] + step_size * tendency
                na_ref[c, x] = acc
                nv_ref[c, x] = v_ref[c, x] + update_rate * acc

    shape = jax.ShapeDtypeStruct(velocity.shape, jnp.float32)
    return pl.pallas_call(kernel, out_shape=(shape, shape))(velocity, accumulated, local_terms, back)


def shards(
    velocity, accumulated, wall_first, wall_second, recycle_rows, weight_index, weight_table
):
    comps, planes, rows_here, span = velocity.shape
    parts = lax.axis_size("ga")
    share = span // parts
    rows = rows_here * parts
    width = comps * planes * share

    send = pack_columns(velocity, parts)
    cols = lax.all_to_all(send, "ga", 0, 0, tiled=True).reshape(rows, width)
    mix = interpolation_matrix(recycle_rows, weight_index, weight_table, rows)
    mix, halo_source = lax.optimization_barrier((mix, velocity))
    behind, ahead = halo_planes(halo_source)
    cols, mix, span_source = lax.optimization_barrier((cols, mix, velocity))

    source_slab, source_plane = divmod(RECYCLE_PLANE, planes)
    plane = jnp.concatenate(
        [cols[:, (c * planes + source_plane) * share : (c * planes + source_plane + 1) * share] for c in range(comps)],
        axis=1,
    )
    inflow = jnp.dot(mix, plane, precision=HIGHEST, preferred_element_type=jnp.float32)
    inflow = lax.ppermute(inflow, "gx", [(source_slab, 0)])

    wall = wall_block(cols, wall_first, wall_second, planes)
    lines = span_source.reshape(-1, span)
    spectral = jnp.dot(
        lines,
        jnp.asarray(spanwise_table(span)),
        precision=HIGHEST,
        preferred_element_type=jnp.float32,
    )
    span_first = spectral[:, :span].reshape(velocity.shape)
    span_second = spectral[:, span:].reshape(velocity.shape)
    span_terms = -(span_source[2:3] * span_first) + viscosity * span_second
    inflow, wall, span_terms = lax.optimization_barrier((inflow, wall, span_terms))

    inlet = (lax.axis_index("gx") == 0).astype(jnp.int32).reshape(1)
    wall = add_ghost(wall, cols, inflow, inlet, planes)
    back = lax.all_to_all(wall.reshape(parts, rows_here, width), "ga", 0, 0, tiled=True)

    local_terms = span_terms + streamwise(velocity, behind, ahead)
    return combine(velocity, accumulated, local_terms, back)


def solution(mesh):
    in_specs = (P(None, "gx", "ga", None), P(None, "gx", "ga", None), P(), P(), P(), P(), P())
    out_specs = (P(None, "gx", "ga", None), P(None, "gx", "ga", None))
    return jax.shard_map(shards, mesh=mesh, in_specs=in_specs, out_specs=out_specs, check_vma=False)
```

```python
import math

import numpy as np
import jax
import jax.numpy as jnp
from jax import lax
from jax.experimental import pallas as pl
from jax.experimental.pallas import tpu as pltpu
from jax.sharding import PartitionSpec as P

HALO = 4
RECYCLE_PLANE = 124


first_coef = (0.8, -0.2, 4.0 / 105.0, -1.0 / 280.0)
second_coef = (1.6, -0.2, 8.0 / 315.0, -1.0 / 560.0)
center_coef = -205.0 / 72.0
step_size = 0.2
viscosity = 0.2
keep_rate = -5.0 / 9.0
update_rate = 15.0 / 16.0
HIGHEST = lax.Precision.HIGHEST


def spanwise_table(length):
    places = np.arange(length)
    apart = places[None, :] - places[:, None]
    apart = np.remainder(apart + length // 2, length) - length // 2
    parity = 1.0 - 2.0 * np.remainder(apart, 2)
    spacing = 2.0 * math.pi / length
    angle = apart * (0.5 * spacing)
    same = apart == 0
    safe_sine = np.where(same, 1.0, np.sin(angle))
    first = np.where(same, 0.0, 0.5 * spacing * parity * np.cos(angle) / safe_sine)
    second = np.where(
        same,
        -math.pi * math.pi / 3.0 - spacing * spacing / 6.0,
        -0.5 * spacing * spacing * parity / (safe_sine * safe_sine),
    )
    return np.concatenate([first, second], 1).astype(np.float32)


def ghost_weights(planes):
    lower = [sum(first_coef[m - 1] for m in range(x + 1, HALO + 1)) for x in range(planes)]
    upper = [sum(second_coef[m - 1] for m in range(x + 1, HALO + 1)) for x in range(planes)]
    return np.asarray(lower, np.float32), np.asarray(upper, np.float32)


def halo_planes(field):
    count = lax.axis_size("gx")
    behind = lax.ppermute(field, "gx", [(i, i + 1) for i in range(count - 1)])
    ahead = lax.ppermute(field, "gx", [(i + 1, i) for i in range(count - 1)])
    return behind, ahead


def streamwise(field, behind, ahead):
    count = lax.axis_size("gx")
    extent = field.shape[1]
    at_outlet = lax.axis_index("gx") == count - 1
    ahead = jnp.where(at_outlet, jnp.broadcast_to(field[:, -1:], ahead.shape), ahead)
    padded = jnp.concatenate([behind[:, extent - HALO :], field, ahead[:, :HALO]], 1)
    first = jnp.zeros_like(field)
    second = center_coef * field
    for offset in range(1, HALO + 1):
        up = padded[:, HALO + offset : HALO + offset + extent]
        down = padded[:, HALO - offset : HALO - offset + extent]
        first = first + first_coef[offset - 1] * (up - down)
        second = second + second_coef[offset - 1] * (up + down)
    return -(field[0:1] * first) + viscosity * second


def interpolation_matrix(recycle_rows, weight_index, weight_table, rows):
    levels = jnp.arange(weight_table.shape[0], dtype=jnp.int32)
    frac = jnp.sum(
        jnp.where(weight_index[:, None] == levels[None, :], weight_table[None, :], 0.0), axis=1
    )[:, None]
    places = jnp.arange(rows, dtype=jnp.int32)[None, :]
    lower = jnp.where(places == recycle_rows[:, None], 1.0 - frac, 0.0)
    upper = jnp.where(places == recycle_rows[:, None] + 1, frac, 0.0)
    return lower + upper


def pack_columns(velocity, parts):
    comps, planes, rows_here, span = velocity.shape
    share = span // parts

    def kernel(v_ref, o_ref):
        for d in range(parts):
            pieces = [
                v_ref[c, x, :, share * d : share * (d + 1)] for c in range(comps) for x in range(planes)
            ]
            o_ref[d] = jnp.concatenate(pieces, axis=1)

    return pl.pallas_call(
        kernel,
        out_shape=jax.ShapeDtypeStruct((parts, rows_here, comps * planes * share), jnp.float32),
    )(velocity)


def wall_block(cols, wall_first, wall_second, planes):
    rows, width = cols.shape
    comps = 3
    block = width // comps

    def kernel(c_ref, f_ref, s_ref, o_ref):
        field = c_ref[...]
        first = jnp.dot(f_ref[...], field, precision=HIGHEST, preferred_element_type=jnp.float32)
        second = jnp.dot(s_ref[...], field, precision=HIGHEST, preferred_element_type=jnp.float32)
        v1 = c_ref[:, block : 2 * block]
        for c in range(comps):
            part = slice(c * block, (c + 1) * block)
            o_ref[:, part] = -(v1 * first[:, part]) + viscosity * second[:, part]

    return pl.pallas_call(kernel, out_shape=jax.ShapeDtypeStruct((rows, width), jnp.float32))(
        cols, wall_first, wall_second
    )


def add_ghost(wall, cols, inflow, inlet, planes):
    rows, width = cols.shape
    comps = 3
    share = width // (comps * planes)
    block = planes * share
    lower, upper = ghost_weights(planes)
    gain = np.tile(np.repeat(lower, share), comps)[None, :]
    bias = np.tile(np.repeat(viscosity * upper, share), comps)[None, :]

    def kernel(inlet_ref, w_ref, c_ref, f_ref, g_ref, b_ref, o_ref):
        at_inlet = inlet_ref[0] > 0

        @pl.when(at_inlet)
        def _():
            flow = jnp.concatenate(
                [f_ref[:, c * share : (c + 1) * share] for c in range(comps) for x in range(planes)],
                axis=1,
            )
            first = c_ref[:, 0:block]
            spread = jnp.concatenate([first] * comps, axis=1)
            o_ref[...] = w_ref[...] + flow * (spread * g_ref[...] + b_ref[...])

        @pl.when(jnp.logical_not(at_inlet))
        def _():
            o_ref[...] = w_ref[...]

    vmem = pl.BlockSpec(memory_space=pltpu.VMEM)
    return pl.pallas_call(
        kernel,
        out_shape=jax.ShapeDtypeStruct((rows, width), jnp.float32),
        in_specs=[pl.BlockSpec(memory_space=pltpu.SMEM)] + [vmem] * 5,
        input_output_aliases={1: 0},
    )(inlet, wall, cols, inflow, jnp.asarray(gain, jnp.float32), jnp.asarray(bias, jnp.float32))


def combine(velocity, accumulated, local_terms, back):
    comps, planes, rows_here, span = velocity.shape
    parts = back.shape[0]
    share = span // parts

    def kernel(v_ref, a_ref, t_ref, b_ref, nv_ref, na_ref):
        for c in range(comps):
            for x in range(planes):
                k = (c * planes + x) * share
                wall = jnp.concatenate([b_ref[d, :, k : k + share] for d in range(parts)], axis=1)
                tendency = t_ref[c, x] + wall
                acc = keep_rate * a_ref[c, x] + step_size * tendency
                na_ref[c, x] = acc
                nv_ref[c, x] = v_ref[c, x] + update_rate * acc

    shape = jax.ShapeDtypeStruct(velocity.shape, jnp.float32)
    return pl.pallas_call(kernel, out_shape=(shape, shape))(velocity, accumulated, local_terms, back)


def shards(
    velocity, accumulated, wall_first, wall_second, recycle_rows, weight_index, weight_table
):
    comps, planes, rows_here, span = velocity.shape
    parts = lax.axis_size("ga")
    share = span // parts
    rows = rows_here * parts
    width = comps * planes * share

    send = pack_columns(velocity, parts)
    cols = lax.all_to_all(send, "ga", 0, 0, tiled=True).reshape(rows, width)
    mix = interpolation_matrix(recycle_rows, weight_index, weight_table, rows)
    mix, halo_source = lax.optimization_barrier((mix, velocity))
    behind, ahead = halo_planes(halo_source)
    cols, mix, span_source = lax.optimization_barrier((cols, mix, velocity))

    source_slab, source_plane = divmod(RECYCLE_PLANE, planes)
    plane = jnp.concatenate(
        [cols[:, (c * planes + source_plane) * share : (c * planes + source_plane + 1) * share] for c in range(comps)],
        axis=1,
    )
    inflow = jnp.dot(mix, plane, precision=HIGHEST, preferred_element_type=jnp.float32)
    inflow = lax.ppermute(inflow, "gx", [(source_slab, 0)])

    wall = wall_block(cols, wall_first, wall_second, planes)
    lines = span_source.reshape(-1, span)
    spectral = jnp.dot(
        lines,
        jnp.asarray(spanwise_table(span)),
        precision=HIGHEST,
        preferred_element_type=jnp.float32,
    )
    span_first = spectral[:, :span].reshape(velocity.shape)
    span_second = spectral[:, span:].reshape(velocity.shape)
    span_terms = -(span_source[2:3] * span_first) + viscosity * span_second
    inflow, wall, span_terms = lax.optimization_barrier((inflow, wall, span_terms))

    inlet = (lax.axis_index("gx") == 0).astype(jnp.int32).reshape(1)
    wall = add_ghost(wall, cols, inflow, inlet, planes)
    back = lax.all_to_all(wall.reshape(parts, rows_here, width), "ga", 0, 0, tiled=True)

    local_terms = span_terms + streamwise(velocity, behind, ahead)
    return combine(velocity, accumulated, local_terms, back)


def solution(mesh):
    in_specs = (P(None, "gx", "ga", None), P(None, "gx", "ga", None), P(), P(), P(), P(), P())
    out_specs = (P(None, "gx", "ga", None), P(None, "gx", "ga", None))
    return jax.shard_map(shards, mesh=mesh, in_specs=in_specs, out_specs=out_specs, check_vma=False)
```

```python
import math

import numpy as np
import jax
import jax.numpy as jnp
from jax import lax
from jax.experimental import pallas as pl
from jax.experimental.pallas import tpu as pltpu
from jax.sharding import PartitionSpec as P

HALO = 4
RECYCLE_PLANE = 124


first_coef = (0.8, -0.2, 4.0 / 105.0, -1.0 / 280.0)
second_coef = (1.6, -0.2, 8.0 / 315.0, -1.0 / 560.0)
center_coef = -205.0 / 72.0
step_size = 0.2
viscosity = 0.2
keep_rate = -5.0 / 9.0
update_rate = 15.0 / 16.0
HIGHEST = lax.Precision.HIGHEST


def spanwise_table(length):
    places = np.arange(length)
    apart = places[None, :] - places[:, None]
    apart = np.remainder(apart + length // 2, length) - length // 2
    parity = 1.0 - 2.0 * np.remainder(apart, 2)
    spacing = 2.0 * math.pi / length
    angle = apart * (0.5 * spacing)
    same = apart == 0
    safe_sine = np.where(same, 1.0, np.sin(angle))
    first = np.where(same, 0.0, 0.5 * spacing * parity * np.cos(angle) / safe_sine)
    second = np.where(
        same,
        -math.pi * math.pi / 3.0 - spacing * spacing / 6.0,
        -0.5 * spacing * spacing * parity / (safe_sine * safe_sine),
    )
    return np.concatenate([first, second], 1).astype(np.float32)


def ghost_weights(planes):
    lower = [sum(first_coef[m - 1] for m in range(x + 1, HALO + 1)) for x in range(planes)]
    upper = [sum(second_coef[m - 1] for m in range(x + 1, HALO + 1)) for x in range(planes)]
    return np.asarray(lower, np.float32), np.asarray(upper, np.float32)


def halo_planes(field):
    count = lax.axis_size("gx")
    behind = lax.ppermute(field, "gx", [(i, i + 1) for i in range(count - 1)])
    ahead = lax.ppermute(field, "gx", [(i + 1, i) for i in range(count - 1)])
    return behind, ahead


def streamwise(field, behind, ahead):
    count = lax.axis_size("gx")
    extent = field.shape[1]
    at_outlet = lax.axis_index("gx") == count - 1
    ahead = jnp.where(at_outlet, jnp.broadcast_to(field[:, -1:], ahead.shape), ahead)
    padded = jnp.concatenate([behind[:, extent - HALO :], field, ahead[:, :HALO]], 1)
    first = jnp.zeros_like(field)
    second = center_coef * field
    for offset in range(1, HALO + 1):
        up = padded[:, HALO + offset : HALO + offset + extent]
        down = padded[:, HALO - offset : HALO - offset + extent]
        first = first + first_coef[offset - 1] * (up - down)
        second = second + second_coef[offset - 1] * (up + down)
    return -(field[0:1] * first) + viscosity * second


def interpolation_matrix(recycle_rows, weight_index, weight_table, rows):
    levels = jnp.arange(weight_table.shape[0], dtype=jnp.int32)
    frac = jnp.sum(
        jnp.where(weight_index[:, None] == levels[None, :], weight_table[None, :], 0.0), axis=1
    )[:, None]
    places = jnp.arange(rows, dtype=jnp.int32)[None, :]
    lower = jnp.where(places == recycle_rows[:, None], 1.0 - frac, 0.0)
    upper = jnp.where(places == recycle_rows[:, None] + 1, frac, 0.0)
    return lower + upper


def pack_columns(velocity, parts):
    comps, planes, rows_here, span = velocity.shape
    share = span // parts

    def kernel(v_ref, o_ref):
        for d in range(parts):
            pieces = [
                v_ref[c, x, :, share * d : share * (d + 1)] for c in range(comps) for x in range(planes)
            ]
            o_ref[d] = jnp.concatenate(pieces, axis=1)

    return pl.pallas_call(
        kernel,
        out_shape=jax.ShapeDtypeStruct((parts, rows_here, comps * planes * share), jnp.float32),
    )(velocity)


def wall_block(cols, wall_first, wall_second, planes):
    rows, width = cols.shape
    comps = 3
    block = width // comps

    def kernel(c_ref, f_ref, s_ref, o_ref):
        field = c_ref[...]
        first = jnp.dot(f_ref[...], field, precision=HIGHEST, preferred_element_type=jnp.float32)
        second = jnp.dot(s_ref[...], field, precision=HIGHEST, preferred_element_type=jnp.float32)
        v1 = c_ref[:, block : 2 * block]
        for c in range(comps):
            part = slice(c * block, (c + 1) * block)
            o_ref[:, part] = -(v1 * first[:, part]) + viscosity * second[:, part]

    return pl.pallas_call(kernel, out_shape=jax.ShapeDtypeStruct((rows, width), jnp.float32))(
        cols, wall_first, wall_second
    )


def add_ghost(wall, cols, inflow, inlet, planes):
    rows, width = cols.shape
    comps = 3
    share = width // (comps * planes)
    block = planes * share
    lower, upper = ghost_weights(planes)
    gain = np.tile(np.repeat(lower, share), comps)[None, :]
    bias = np.tile(np.repeat(viscosity * upper, share), comps)[None, :]

    def kernel(inlet_ref, w_ref, c_ref, f_ref, g_ref, b_ref, o_ref):
        at_inlet = inlet_ref[0] > 0

        @pl.when(at_inlet)
        def _():
            flow = jnp.concatenate(
                [f_ref[:, c * share : (c + 1) * share] for c in range(comps) for x in range(planes)],
                axis=1,
            )
            first = c_ref[:, 0:block]
            spread = jnp.concatenate([first] * comps, axis=1)
            o_ref[...] = w_ref[...] + flow * (spread * g_ref[...] + b_ref[...])

        @pl.when(jnp.logical_not(at_inlet))
        def _():
            o_ref[...] = w_ref[...]

    vmem = pl.BlockSpec(memory_space=pltpu.VMEM)
    return pl.pallas_call(
        kernel,
        out_shape=jax.ShapeDtypeStruct((rows, width), jnp.float32),
        in_specs=[pl.BlockSpec(memory_space=pltpu.SMEM)] + [vmem] * 5,
        input_output_aliases={1: 0},
    )(inlet, wall, cols, inflow, jnp.asarray(gain, jnp.float32), jnp.asarray(bias, jnp.float32))


def combine(velocity, accumulated, local_terms, back):
    comps, planes, rows_here, span = velocity.shape
    parts = back.shape[0]
    share = span // parts

    def kernel(v_ref, a_ref, t_ref, b_ref, nv_ref, na_ref):
        for c in range(comps):
            for x in range(planes):
                k = (c * planes + x) * share
                wall = jnp.concatenate([b_ref[d, :, k : k + share] for d in range(parts)], axis=1)
                tendency = t_ref[c, x] + wall
                acc = keep_rate * a_ref[c, x] + step_size * tendency
                na_ref[c, x] = acc
                nv_ref[c, x] = v_ref[c, x] + update_rate * acc

    shape = jax.ShapeDtypeStruct(velocity.shape, jnp.float32)
    return pl.pallas_call(kernel, out_shape=(shape, shape))(velocity, accumulated, local_terms, back)


def shards(
    velocity, accumulated, wall_first, wall_second, recycle_rows, weight_index, weight_table
):
    comps, planes, rows_here, span = velocity.shape
    parts = lax.axis_size("ga")
    share = span // parts
    rows = rows_here * parts
    width = comps * planes * share

    send = pack_columns(velocity, parts)
    cols = lax.all_to_all(send, "ga", 0, 0, tiled=True).reshape(rows, width)
    mix = interpolation_matrix(recycle_rows, weight_index, weight_table, rows)
    mix, halo_source = lax.optimization_barrier((mix, velocity))
    behind, ahead = halo_planes(halo_source)
    cols, mix, span_source, behind, ahead = lax.optimization_barrier((cols, mix, velocity, behind, ahead))

    source_slab, source_plane = divmod(RECYCLE_PLANE, planes)
    plane = jnp.concatenate(
        [cols[:, (c * planes + source_plane) * share : (c * planes + source_plane + 1) * share] for c in range(comps)],
        axis=1,
    )
    inflow = jnp.dot(mix, plane, precision=HIGHEST, preferred_element_type=jnp.float32)
    inflow = lax.ppermute(inflow, "gx", [(source_slab, 0)])

    wall = wall_block(cols, wall_first, wall_second, planes)
    lines = span_source.reshape(-1, span)
    spectral = jnp.dot(
        lines,
        jnp.asarray(spanwise_table(span)),
        precision=HIGHEST,
        preferred_element_type=jnp.float32,
    )
    span_first = spectral[:, :span].reshape(velocity.shape)
    span_second = spectral[:, span:].reshape(velocity.shape)
    span_terms = -(span_source[2:3] * span_first) + viscosity * span_second
    inflow, wall, span_terms = lax.optimization_barrier((inflow, wall, span_terms))

    inlet = (lax.axis_index("gx") == 0).astype(jnp.int32).reshape(1)
    wall = add_ghost(wall, cols, inflow, inlet, planes)
    back = lax.all_to_all(wall.reshape(parts, rows_here, width), "ga", 0, 0, tiled=True)

    local_terms = span_terms + streamwise(velocity, behind, ahead)
    return combine(velocity, accumulated, local_terms, back)


def solution(mesh):
    in_specs = (P(None, "gx", "ga", None), P(None, "gx", "ga", None), P(), P(), P(), P(), P())
    out_specs = (P(None, "gx", "ga", None), P(None, "gx", "ga", None))
    return jax.shard_map(shards, mesh=mesh, in_specs=in_specs, out_specs=out_specs, check_vma=False)
```

```python
import math

import numpy as np
import jax
import jax.numpy as jnp
from jax import lax
from jax.experimental import pallas as pl
from jax.experimental.pallas import tpu as pltpu
from jax.sharding import PartitionSpec as P

HALO = 4
RECYCLE_PLANE = 124


first_coef = (0.8, -0.2, 4.0 / 105.0, -1.0 / 280.0)
second_coef = (1.6, -0.2, 8.0 / 315.0, -1.0 / 560.0)
center_coef = -205.0 / 72.0
step_size = 0.2
viscosity = 0.2
keep_rate = -5.0 / 9.0
update_rate = 15.0 / 16.0
HIGHEST = lax.Precision.HIGHEST


def spanwise_table(length):
    places = np.arange(length)
    apart = places[None, :] - places[:, None]
    apart = np.remainder(apart + length // 2, length) - length // 2
    parity = 1.0 - 2.0 * np.remainder(apart, 2)
    spacing = 2.0 * math.pi / length
    angle = apart * (0.5 * spacing)
    same = apart == 0
    safe_sine = np.where(same, 1.0, np.sin(angle))
    first = np.where(same, 0.0, 0.5 * spacing * parity * np.cos(angle) / safe_sine)
    second = np.where(
        same,
        -math.pi * math.pi / 3.0 - spacing * spacing / 6.0,
        -0.5 * spacing * spacing * parity / (safe_sine * safe_sine),
    )
    return np.concatenate([first, second], 1).astype(np.float32)


def ghost_weights(planes):
    lower = [sum(first_coef[m - 1] for m in range(x + 1, HALO + 1)) for x in range(planes)]
    upper = [sum(second_coef[m - 1] for m in range(x + 1, HALO + 1)) for x in range(planes)]
    return np.asarray(lower, np.float32), np.asarray(upper, np.float32)


def halo_planes(field):
    count = lax.axis_size("gx")
    behind = lax.ppermute(field, "gx", [(i, i + 1) for i in range(count - 1)])
    ahead = lax.ppermute(field, "gx", [(i + 1, i) for i in range(count - 1)])
    return behind, ahead


def streamwise(field, behind, ahead):
    count = lax.axis_size("gx")
    extent = field.shape[1]
    at_outlet = lax.axis_index("gx") == count - 1
    ahead = jnp.where(at_outlet, jnp.broadcast_to(field[:, -1:], ahead.shape), ahead)
    padded = jnp.concatenate([behind[:, extent - HALO :], field, ahead[:, :HALO]], 1)
    first = jnp.zeros_like(field)
    second = center_coef * field
    for offset in range(1, HALO + 1):
        up = padded[:, HALO + offset : HALO + offset + extent]
        down = padded[:, HALO - offset : HALO - offset + extent]
        first = first + first_coef[offset - 1] * (up - down)
        second = second + second_coef[offset - 1] * (up + down)
    return -(field[0:1] * first) + viscosity * second


def interpolation_matrix(recycle_rows, weight_index, weight_table, rows):
    levels = jnp.arange(weight_table.shape[0], dtype=jnp.int32)
    frac = jnp.sum(
        jnp.where(weight_index[:, None] == levels[None, :], weight_table[None, :], 0.0), axis=1
    )[:, None]
    places = jnp.arange(rows, dtype=jnp.int32)[None, :]
    lower = jnp.where(places == recycle_rows[:, None], 1.0 - frac, 0.0)
    upper = jnp.where(places == recycle_rows[:, None] + 1, frac, 0.0)
    return lower + upper


def pack_columns(velocity, parts):
    comps, planes, rows_here, span = velocity.shape
    share = span // parts

    def kernel(v_ref, o_ref):
        for d in range(parts):
            pieces = [
                v_ref[c, x, :, share * d : share * (d + 1)] for c in range(comps) for x in range(planes)
            ]
            o_ref[d] = jnp.concatenate(pieces, axis=1)

    return pl.pallas_call(
        kernel,
        out_shape=jax.ShapeDtypeStruct((parts, rows_here, comps * planes * share), jnp.float32),
    )(velocity)


def wall_block(cols, wall_first, wall_second, planes):
    rows, width = cols.shape
    comps = 3
    block = width // comps

    def kernel(c_ref, f_ref, s_ref, o_ref):
        field = c_ref[...]
        first = jnp.dot(f_ref[...], field, precision=HIGHEST, preferred_element_type=jnp.float32)
        second = jnp.dot(s_ref[...], field, precision=HIGHEST, preferred_element_type=jnp.float32)
        v1 = c_ref[:, block : 2 * block]
        for c in range(comps):
            part = slice(c * block, (c + 1) * block)
            o_ref[:, part] = -(v1 * first[:, part]) + viscosity * second[:, part]

    return pl.pallas_call(kernel, out_shape=jax.ShapeDtypeStruct((rows, width), jnp.float32))(
        cols, wall_first, wall_second
    )


def add_ghost(wall, cols, inflow, inlet, planes):
    rows, width = cols.shape
    comps = 3
    share = width // (comps * planes)
    block = planes * share
    lower, upper = ghost_weights(planes)
    gain = np.tile(np.repeat(lower, share), comps)[None, :]
    bias = np.tile(np.repeat(viscosity * upper, share), comps)[None, :]

    def kernel(inlet_ref, w_ref, c_ref, f_ref, g_ref, b_ref, o_ref):
        at_inlet = inlet_ref[0] > 0

        @pl.when(at_inlet)
        def _():
            flow = jnp.concatenate(
                [f_ref[:, c * share : (c + 1) * share] for c in range(comps) for x in range(planes)],
                axis=1,
            )
            first = c_ref[:, 0:block]
            spread = jnp.concatenate([first] * comps, axis=1)
            o_ref[...] = w_ref[...] + flow * (spread * g_ref[...] + b_ref[...])

        @pl.when(jnp.logical_not(at_inlet))
        def _():
            o_ref[...] = w_ref[...]

    vmem = pl.BlockSpec(memory_space=pltpu.VMEM)
    return pl.pallas_call(
        kernel,
        out_shape=jax.ShapeDtypeStruct((rows, width), jnp.float32),
        in_specs=[pl.BlockSpec(memory_space=pltpu.SMEM)] + [vmem] * 5,
        input_output_aliases={1: 0},
    )(inlet, wall, cols, inflow, jnp.asarray(gain, jnp.float32), jnp.asarray(bias, jnp.float32))


def combine(velocity, accumulated, local_terms, back):
    comps, planes, rows_here, span = velocity.shape
    parts = back.shape[0]
    share = span // parts

    partial = keep_rate * accumulated + step_size * local_terms

    def kernel(v_ref, p_ref, b_ref, nv_ref, na_ref):
        for c in range(comps):
            for x in range(planes):
                k = (c * planes + x) * share
                wall = jnp.concatenate([b_ref[d, :, k : k + share] for d in range(parts)], axis=1)
                acc = p_ref[c, x] + step_size * wall
                na_ref[c, x] = acc
                nv_ref[c, x] = v_ref[c, x] + update_rate * acc

    shape = jax.ShapeDtypeStruct(velocity.shape, jnp.float32)
    return pl.pallas_call(kernel, out_shape=(shape, shape))(velocity, partial, back)


def shards(
    velocity, accumulated, wall_first, wall_second, recycle_rows, weight_index, weight_table
):
    comps, planes, rows_here, span = velocity.shape
    parts = lax.axis_size("ga")
    share = span // parts
    rows = rows_here * parts
    width = comps * planes * share

    send = pack_columns(velocity, parts)
    cols = lax.all_to_all(send, "ga", 0, 0, tiled=True).reshape(rows, width)
    mix = interpolation_matrix(recycle_rows, weight_index, weight_table, rows)
    mix, halo_source = lax.optimization_barrier((mix, velocity))
    behind, ahead = halo_planes(halo_source)
    cols, mix, span_source = lax.optimization_barrier((cols, mix, velocity))

    source_slab, source_plane = divmod(RECYCLE_PLANE, planes)
    plane = jnp.concatenate(
        [cols[:, (c * planes + source_plane) * share : (c * planes + source_plane + 1) * share] for c in range(comps)],
        axis=1,
    )
    inflow = jnp.dot(mix, plane, precision=HIGHEST, preferred_element_type=jnp.float32)
    inflow = lax.ppermute(inflow, "gx", [(source_slab, 0)])

    wall = wall_block(cols, wall_first, wall_second, planes)
    lines = span_source.reshape(-1, span)
    spectral = jnp.dot(
        lines,
        jnp.asarray(spanwise_table(span)),
        precision=HIGHEST,
        preferred_element_type=jnp.float32,
    )
    span_first = spectral[:, :span].reshape(velocity.shape)
    span_second = spectral[:, span:].reshape(velocity.shape)
    span_terms = -(span_source[2:3] * span_first) + viscosity * span_second
    inflow, wall, span_terms = lax.optimization_barrier((inflow, wall, span_terms))

    inlet = (lax.axis_index("gx") == 0).astype(jnp.int32).reshape(1)
    wall = add_ghost(wall, cols, inflow, inlet, planes)
    back = lax.all_to_all(wall.reshape(parts, rows_here, width), "ga", 0, 0, tiled=True)

    local_terms = span_terms + streamwise(velocity, behind, ahead)
    return combine(velocity, accumulated, local_terms, back)


def solution(mesh):
    in_specs = (P(None, "gx", "ga", None), P(None, "gx", "ga", None), P(), P(), P(), P(), P())
    out_specs = (P(None, "gx", "ga", None), P(None, "gx", "ga", None))
    return jax.shard_map(shards, mesh=mesh, in_specs=in_specs, out_specs=out_specs, check_vma=False)
```

```python
import math

import numpy as np
import jax
import jax.numpy as jnp
from jax import lax
from jax.experimental import pallas as pl
from jax.experimental.pallas import tpu as pltpu
from jax.sharding import PartitionSpec as P

HALO = 4
RECYCLE_PLANE = 124


first_coef = (0.8, -0.2, 4.0 / 105.0, -1.0 / 280.0)
second_coef = (1.6, -0.2, 8.0 / 315.0, -1.0 / 560.0)
center_coef = -205.0 / 72.0
step_size = 0.2
viscosity = 0.2
keep_rate = -5.0 / 9.0
update_rate = 15.0 / 16.0
HIGHEST = lax.Precision.HIGHEST


def spanwise_table(length):
    places = np.arange(length)
    apart = places[None, :] - places[:, None]
    apart = np.remainder(apart + length // 2, length) - length // 2
    parity = 1.0 - 2.0 * np.remainder(apart, 2)
    spacing = 2.0 * math.pi / length
    angle = apart * (0.5 * spacing)
    same = apart == 0
    safe_sine = np.where(same, 1.0, np.sin(angle))
    first = np.where(same, 0.0, 0.5 * spacing * parity * np.cos(angle) / safe_sine)
    second = np.where(
        same,
        -math.pi * math.pi / 3.0 - spacing * spacing / 6.0,
        -0.5 * spacing * spacing * parity / (safe_sine * safe_sine),
    )
    return np.concatenate([first, second], 1).astype(np.float32)


def ghost_weights(planes):
    lower = [sum(first_coef[m - 1] for m in range(x + 1, HALO + 1)) for x in range(planes)]
    upper = [sum(second_coef[m - 1] for m in range(x + 1, HALO + 1)) for x in range(planes)]
    return np.asarray(lower, np.float32), np.asarray(upper, np.float32)


def halo_planes(field):
    count = lax.axis_size("gx")
    behind = lax.ppermute(field, "gx", [(i, i + 1) for i in range(count - 1)])
    ahead = lax.ppermute(field, "gx", [(i + 1, i) for i in range(count - 1)])
    return behind, ahead


def streamwise(field, behind, ahead):
    count = lax.axis_size("gx")
    extent = field.shape[1]
    at_outlet = lax.axis_index("gx") == count - 1
    ahead = jnp.where(at_outlet, jnp.broadcast_to(field[:, -1:], ahead.shape), ahead)
    padded = jnp.concatenate([behind[:, extent - HALO :], field, ahead[:, :HALO]], 1)
    first = jnp.zeros_like(field)
    second = center_coef * field
    for offset in range(1, HALO + 1):
        up = padded[:, HALO + offset : HALO + offset + extent]
        down = padded[:, HALO - offset : HALO - offset + extent]
        first = first + first_coef[offset - 1] * (up - down)
        second = second + second_coef[offset - 1] * (up + down)
    return -(field[0:1] * first) + viscosity * second


def interpolation_matrix(recycle_rows, weight_index, weight_table, rows):
    levels = jnp.arange(weight_table.shape[0], dtype=jnp.int32)
    frac = jnp.sum(
        jnp.where(weight_index[:, None] == levels[None, :], weight_table[None, :], 0.0), axis=1
    )[:, None]
    places = jnp.arange(rows, dtype=jnp.int32)[None, :]
    lower = jnp.where(places == recycle_rows[:, None], 1.0 - frac, 0.0)
    upper = jnp.where(places == recycle_rows[:, None] + 1, frac, 0.0)
    return lower + upper


def pack_columns(velocity, parts):
    comps, planes, rows_here, span = velocity.shape
    share = span // parts

    def kernel(v_ref, o_ref):
        for d in range(parts):
            pieces = [
                v_ref[c, x, :, share * d : share * (d + 1)] for c in range(comps) for x in range(planes)
            ]
            o_ref[d] = jnp.concatenate(pieces, axis=1)

    return pl.pallas_call(
        kernel,
        out_shape=jax.ShapeDtypeStruct((parts, rows_here, comps * planes * share), jnp.float32),
    )(velocity)


def wall_block(cols, wall_first, wall_second, planes):
    rows, width = cols.shape
    comps = 3
    block = width // comps

    def kernel(c_ref, f_ref, s_ref, o_ref):
        field = c_ref[...]
        first = jnp.dot(f_ref[...], field, precision=HIGHEST, preferred_element_type=jnp.float32)
        second = jnp.dot(s_ref[...], field, precision=HIGHEST, preferred_element_type=jnp.float32)
        v1 = c_ref[:, block : 2 * block]
        for c in range(comps):
            part = slice(c * block, (c + 1) * block)
            o_ref[:, part] = -(v1 * first[:, part]) + viscosity * second[:, part]

    return pl.pallas_call(kernel, out_shape=jax.ShapeDtypeStruct((rows, width), jnp.float32))(
        cols, wall_first, wall_second
    )


def add_ghost(wall, cols, inflow, inlet, planes):
    rows, width = cols.shape
    comps = 3
    share = width // (comps * planes)
    block = planes * share
    lower, upper = ghost_weights(planes)
    gain = np.tile(np.repeat(lower, share), comps)[None, :]
    bias = np.tile(np.repeat(viscosity * upper, share), comps)[None, :]

    def kernel(inlet_ref, w_ref, c_ref, f_ref, g_ref, b_ref, o_ref):
        at_inlet = inlet_ref[0] > 0

        @pl.when(at_inlet)
        def _():
            flow = jnp.concatenate(
                [f_ref[:, c * share : (c + 1) * share] for c in range(comps) for x in range(planes)],
                axis=1,
            )
            first = c_ref[:, 0:block]
            spread = jnp.concatenate([first] * comps, axis=1)
            o_ref[...] = w_ref[...] + flow * (spread * g_ref[...] + b_ref[...])

        @pl.when(jnp.logical_not(at_inlet))
        def _():
            o_ref[...] = w_ref[...]

    vmem = pl.BlockSpec(memory_space=pltpu.VMEM)
    return pl.pallas_call(
        kernel,
        out_shape=jax.ShapeDtypeStruct((rows, width), jnp.float32),
        in_specs=[pl.BlockSpec(memory_space=pltpu.SMEM)] + [vmem] * 5,
        input_output_aliases={1: 0},
    )(inlet, wall, cols, inflow, jnp.asarray(gain, jnp.float32), jnp.asarray(bias, jnp.float32))


def combine(velocity, accumulated, local_terms, back):
    comps, planes, rows_here, span = velocity.shape
    parts = back.shape[0]
    share = span // parts

    partial = keep_rate * accumulated + step_size * local_terms

    def kernel(v_ref, p_ref, b_ref, nv_ref, na_ref):
        for c in range(comps):
            for x in range(planes):
                k = (c * planes + x) * share
                wall = jnp.concatenate([b_ref[d, :, k : k + share] for d in range(parts)], axis=1)
                acc = p_ref[c, x] + step_size * wall
                na_ref[c, x] = acc
                nv_ref[c, x] = v_ref[c, x] + update_rate * acc

    shape = jax.ShapeDtypeStruct(velocity.shape, jnp.float32)
    return pl.pallas_call(kernel, out_shape=(shape, shape))(velocity, partial, back)


def shards(
    velocity, accumulated, wall_first, wall_second, recycle_rows, weight_index, weight_table
):
    comps, planes, rows_here, span = velocity.shape
    parts = lax.axis_size("ga")
    share = span // parts
    rows = rows_here * parts
    width = comps * planes * share

    send = pack_columns(velocity, parts)
    cols = lax.all_to_all(send, "ga", 0, 0, tiled=True).reshape(rows, width)
    mix = interpolation_matrix(recycle_rows, weight_index, weight_table, rows)
    mix, halo_source = lax.optimization_barrier((mix, velocity))
    behind, ahead = halo_planes(halo_source)
    cols, mix, span_source = lax.optimization_barrier((cols, mix, velocity))

    source_slab, source_plane = divmod(RECYCLE_PLANE, planes)
    plane = jnp.concatenate(
        [cols[:, (c * planes + source_plane) * share : (c * planes + source_plane + 1) * share] for c in range(comps)],
        axis=1,
    )
    inflow = jnp.dot(mix, plane, precision=HIGHEST, preferred_element_type=jnp.float32)
    inflow = lax.ppermute(inflow, "gx", [(source_slab, 0)])

    wall = wall_block(cols, wall_first, wall_second, planes)
    lines = span_source.reshape(-1, span)
    spectral = jnp.dot(
        lines,
        jnp.asarray(spanwise_table(span)),
        precision=lax.Precision.HIGH,
        preferred_element_type=jnp.float32,
    )
    span_first = spectral[:, :span].reshape(velocity.shape)
    span_second = spectral[:, span:].reshape(velocity.shape)
    span_terms = -(span_source[2:3] * span_first) + viscosity * span_second
    inflow, wall, span_terms = lax.optimization_barrier((inflow, wall, span_terms))

    inlet = (lax.axis_index("gx") == 0).astype(jnp.int32).reshape(1)
    wall = add_ghost(wall, cols, inflow, inlet, planes)
    back = lax.all_to_all(wall.reshape(parts, rows_here, width), "ga", 0, 0, tiled=True)

    local_terms = span_terms + streamwise(velocity, behind, ahead)
    return combine(velocity, accumulated, local_terms, back)


def solution(mesh):
    in_specs = (P(None, "gx", "ga", None), P(None, "gx", "ga", None), P(), P(), P(), P(), P())
    out_specs = (P(None, "gx", "ga", None), P(None, "gx", "ga", None))
    return jax.shard_map(shards, mesh=mesh, in_specs=in_specs, out_specs=out_specs, check_vma=False)
```

```python
import math

import numpy as np
import jax
import jax.numpy as jnp
from jax import lax
from jax.experimental import pallas as pl
from jax.experimental.pallas import tpu as pltpu
from jax.sharding import PartitionSpec as P

HALO = 4
RECYCLE_PLANE = 124


first_coef = (0.8, -0.2, 4.0 / 105.0, -1.0 / 280.0)
second_coef = (1.6, -0.2, 8.0 / 315.0, -1.0 / 560.0)
center_coef = -205.0 / 72.0
step_size = 0.2
viscosity = 0.2
keep_rate = -5.0 / 9.0
update_rate = 15.0 / 16.0
HIGHEST = lax.Precision.HIGHEST


def spanwise_table(length):
    places = np.arange(length)
    apart = places[None, :] - places[:, None]
    apart = np.remainder(apart + length // 2, length) - length // 2
    parity = 1.0 - 2.0 * np.remainder(apart, 2)
    spacing = 2.0 * math.pi / length
    angle = apart * (0.5 * spacing)
    same = apart == 0
    safe_sine = np.where(same, 1.0, np.sin(angle))
    first = np.where(same, 0.0, 0.5 * spacing * parity * np.cos(angle) / safe_sine)
    second = np.where(
        same,
        -math.pi * math.pi / 3.0 - spacing * spacing / 6.0,
        -0.5 * spacing * spacing * parity / (safe_sine * safe_sine),
    )
    return np.concatenate([first, second], 1).astype(np.float32)


def ghost_weights(planes):
    lower = [sum(first_coef[m - 1] for m in range(x + 1, HALO + 1)) for x in range(planes)]
    upper = [sum(second_coef[m - 1] for m in range(x + 1, HALO + 1)) for x in range(planes)]
    return np.asarray(lower, np.float32), np.asarray(upper, np.float32)


def halo_planes(field):
    count = lax.axis_size("gx")
    behind = lax.ppermute(field, "gx", [(i, i + 1) for i in range(count - 1)])
    ahead = lax.ppermute(field, "gx", [(i + 1, i) for i in range(count - 1)])
    return behind, ahead


def streamwise(field, behind, ahead):
    count = lax.axis_size("gx")
    extent = field.shape[1]
    at_outlet = lax.axis_index("gx") == count - 1
    ahead = jnp.where(at_outlet, jnp.broadcast_to(field[:, -1:], ahead.shape), ahead)
    padded = jnp.concatenate([behind[:, extent - HALO :], field, ahead[:, :HALO]], 1)
    first = jnp.zeros_like(field)
    second = center_coef * field
    for offset in range(1, HALO + 1):
        up = padded[:, HALO + offset : HALO + offset + extent]
        down = padded[:, HALO - offset : HALO - offset + extent]
        first = first + first_coef[offset - 1] * (up - down)
        second = second + second_coef[offset - 1] * (up + down)
    return -(field[0:1] * first) + viscosity * second


def interpolation_matrix(recycle_rows, weight_index, weight_table, rows):
    levels = jnp.arange(weight_table.shape[0], dtype=jnp.int32)
    frac = jnp.sum(
        jnp.where(weight_index[:, None] == levels[None, :], weight_table[None, :], 0.0), axis=1
    )[:, None]
    places = jnp.arange(rows, dtype=jnp.int32)[None, :]
    lower = jnp.where(places == recycle_rows[:, None], 1.0 - frac, 0.0)
    upper = jnp.where(places == recycle_rows[:, None] + 1, frac, 0.0)
    return lower + upper


def pack_columns(velocity, parts):
    comps, planes, rows_here, span = velocity.shape
    share = span // parts

    def kernel(v_ref, o_ref):
        for d in range(parts):
            pieces = [
                v_ref[c, x, :, share * d : share * (d + 1)] for c in range(comps) for x in range(planes)
            ]
            o_ref[d] = jnp.concatenate(pieces, axis=1)

    return pl.pallas_call(
        kernel,
        out_shape=jax.ShapeDtypeStruct((parts, rows_here, comps * planes * share), jnp.float32),
    )(velocity)


def wall_block(cols, wall_first, wall_second, planes):
    rows, width = cols.shape
    comps = 3
    block = width // comps

    def kernel(c_ref, f_ref, s_ref, o_ref):
        field = c_ref[...]
        first = jnp.dot(f_ref[...], field, precision=HIGHEST, preferred_element_type=jnp.float32)
        second = jnp.dot(s_ref[...], field, precision=HIGHEST, preferred_element_type=jnp.float32)
        v1 = c_ref[:, block : 2 * block]
        for c in range(comps):
            part = slice(c * block, (c + 1) * block)
            o_ref[:, part] = -(v1 * first[:, part]) + viscosity * second[:, part]

    return pl.pallas_call(kernel, out_shape=jax.ShapeDtypeStruct((rows, width), jnp.float32))(
        cols, wall_first, wall_second
    )


def add_ghost(wall, cols, inflow, inlet, planes):
    rows, width = cols.shape
    comps = 3
    share = width // (comps * planes)
    block = planes * share
    lower, upper = ghost_weights(planes)
    gain = np.tile(np.repeat(lower, share), comps)[None, :]
    bias = np.tile(np.repeat(viscosity * upper, share), comps)[None, :]

    def kernel(inlet_ref, w_ref, c_ref, f_ref, g_ref, b_ref, o_ref):
        at_inlet = inlet_ref[0] > 0

        @pl.when(at_inlet)
        def _():
            flow = jnp.concatenate(
                [f_ref[:, c * share : (c + 1) * share] for c in range(comps) for x in range(planes)],
                axis=1,
            )
            first = c_ref[:, 0:block]
            spread = jnp.concatenate([first] * comps, axis=1)
            o_ref[...] = w_ref[...] + flow * (spread * g_ref[...] + b_ref[...])

        @pl.when(jnp.logical_not(at_inlet))
        def _():
            o_ref[...] = w_ref[...]

    vmem = pl.BlockSpec(memory_space=pltpu.VMEM)
    return pl.pallas_call(
        kernel,
        out_shape=jax.ShapeDtypeStruct((rows, width), jnp.float32),
        in_specs=[pl.BlockSpec(memory_space=pltpu.SMEM)] + [vmem] * 5,
        input_output_aliases={1: 0},
    )(inlet, wall, cols, inflow, jnp.asarray(gain, jnp.float32), jnp.asarray(bias, jnp.float32))


def combine(velocity, accumulated, local_terms, back):
    comps, planes, rows_here, span = velocity.shape
    parts = back.shape[0]
    share = span // parts

    partial = keep_rate * accumulated + step_size * local_terms

    def kernel(v_ref, p_ref, b_ref, nv_ref, na_ref):
        for c in range(comps):
            for x in range(planes):
                k = (c * planes + x) * share
                wall = jnp.concatenate([b_ref[d, :, k : k + share] for d in range(parts)], axis=1)
                acc = p_ref[c, x] + step_size * wall
                na_ref[c, x] = acc
                nv_ref[c, x] = v_ref[c, x] + update_rate * acc

    shape = jax.ShapeDtypeStruct(velocity.shape, jnp.float32)
    return pl.pallas_call(kernel, out_shape=(shape, shape))(velocity, partial, back)


def shards(
    velocity, accumulated, wall_first, wall_second, recycle_rows, weight_index, weight_table
):
    comps, planes, rows_here, span = velocity.shape
    parts = lax.axis_size("ga")
    share = span // parts
    rows = rows_here * parts
    width = comps * planes * share

    send = pack_columns(velocity, parts)
    cols = lax.all_to_all(send, "ga", 0, 0, tiled=True).reshape(rows, width)
    mix = interpolation_matrix(recycle_rows, weight_index, weight_table, rows)
    mix, halo_source = lax.optimization_barrier((mix, velocity))
    behind, ahead = halo_planes(halo_source)
    cols, mix, span_source = lax.optimization_barrier((cols, mix, velocity))

    source_slab, source_plane = divmod(RECYCLE_PLANE, planes)
    plane = jnp.concatenate(
        [cols[:, (c * planes + source_plane) * share : (c * planes + source_plane + 1) * share] for c in range(comps)],
        axis=1,
    )
    inflow = jnp.dot(mix, plane, precision=HIGHEST, preferred_element_type=jnp.float32)
    inflow = lax.ppermute(inflow, "gx", [(source_slab, 0)])

    wall = wall_block(cols, wall_first, wall_second, planes)
    lines = span_source.reshape(-1, span)
    spectral = jnp.dot(
        lines,
        jnp.asarray(spanwise_table(span)),
        precision=lax.Precision.HIGH,
        preferred_element_type=jnp.float32,
    )
    span_first = spectral[:, :span].reshape(velocity.shape)
    span_second = spectral[:, span:].reshape(velocity.shape)
    span_terms = -(span_source[2:3] * span_first) + viscosity * span_second
    inflow, wall, span_terms = lax.optimization_barrier((inflow, wall, span_terms))

    inlet = (lax.axis_index("gx") == 0).astype(jnp.int32).reshape(1)
    lower, upper = ghost_weights(planes)
    gain = jnp.asarray(np.tile(np.repeat(lower, share), comps)[None, :])
    bias = jnp.asarray(np.tile(np.repeat(viscosity * upper, share), comps)[None, :])
    flow = jnp.concatenate(
        [inflow[:, c * share : (c + 1) * share] for c in range(comps) for x in range(planes)], axis=1
    )
    spread = jnp.concatenate([cols[:, 0 : planes * share]] * comps, axis=1)
    wall = wall + jnp.where(inlet[0] > 0, flow * (spread * gain + bias), 0.0)
    back = lax.all_to_all(wall.reshape(parts, rows_here, width), "ga", 0, 0, tiled=True)

    local_terms = span_terms + streamwise(velocity, behind, ahead)
    return combine(velocity, accumulated, local_terms, back)


def solution(mesh):
    in_specs = (P(None, "gx", "ga", None), P(None, "gx", "ga", None), P(), P(), P(), P(), P())
    out_specs = (P(None, "gx", "ga", None), P(None, "gx", "ga", None))
    return jax.shard_map(shards, mesh=mesh, in_specs=in_specs, out_specs=out_specs, check_vma=False)
```

```python
import math

import numpy as np
import jax
import jax.numpy as jnp
from jax import lax
from jax.experimental import pallas as pl
from jax.experimental.pallas import tpu as pltpu
from jax.sharding import PartitionSpec as P

HALO = 4
RECYCLE_PLANE = 124


first_coef = (0.8, -0.2, 4.0 / 105.0, -1.0 / 280.0)
second_coef = (1.6, -0.2, 8.0 / 315.0, -1.0 / 560.0)
center_coef = -205.0 / 72.0
step_size = 0.2
viscosity = 0.2
keep_rate = -5.0 / 9.0
update_rate = 15.0 / 16.0
HIGHEST = lax.Precision.HIGHEST


def spanwise_table(length):
    places = np.arange(length)
    apart = places[None, :] - places[:, None]
    apart = np.remainder(apart + length // 2, length) - length // 2
    parity = 1.0 - 2.0 * np.remainder(apart, 2)
    spacing = 2.0 * math.pi / length
    angle = apart * (0.5 * spacing)
    same = apart == 0
    safe_sine = np.where(same, 1.0, np.sin(angle))
    first = np.where(same, 0.0, 0.5 * spacing * parity * np.cos(angle) / safe_sine)
    second = np.where(
        same,
        -math.pi * math.pi / 3.0 - spacing * spacing / 6.0,
        -0.5 * spacing * spacing * parity / (safe_sine * safe_sine),
    )
    return np.concatenate([first, second], 1).astype(np.float32)


def ghost_weights(planes):
    lower = [sum(first_coef[m - 1] for m in range(x + 1, HALO + 1)) for x in range(planes)]
    upper = [sum(second_coef[m - 1] for m in range(x + 1, HALO + 1)) for x in range(planes)]
    return np.asarray(lower, np.float32), np.asarray(upper, np.float32)


def halo_planes(field):
    count = lax.axis_size("gx")
    behind = lax.ppermute(field, "gx", [(i, i + 1) for i in range(count - 1)])
    ahead = lax.ppermute(field, "gx", [(i + 1, i) for i in range(count - 1)])
    return behind, ahead


def streamwise(field, behind, ahead):
    count = lax.axis_size("gx")
    extent = field.shape[1]
    at_outlet = lax.axis_index("gx") == count - 1
    ahead = jnp.where(at_outlet, jnp.broadcast_to(field[:, -1:], ahead.shape), ahead)
    padded = jnp.concatenate([behind[:, extent - HALO :], field, ahead[:, :HALO]], 1)
    first = jnp.zeros_like(field)
    second = center_coef * field
    for offset in range(1, HALO + 1):
        up = padded[:, HALO + offset : HALO + offset + extent]
        down = padded[:, HALO - offset : HALO - offset + extent]
        first = first + first_coef[offset - 1] * (up - down)
        second = second + second_coef[offset - 1] * (up + down)
    return -(field[0:1] * first) + viscosity * second


def interpolation_matrix(recycle_rows, weight_index, weight_table, rows):
    levels = jnp.arange(weight_table.shape[0], dtype=jnp.int32)
    frac = jnp.sum(
        jnp.where(weight_index[:, None] == levels[None, :], weight_table[None, :], 0.0), axis=1
    )[:, None]
    places = jnp.arange(rows, dtype=jnp.int32)[None, :]
    lower = jnp.where(places == recycle_rows[:, None], 1.0 - frac, 0.0)
    upper = jnp.where(places == recycle_rows[:, None] + 1, frac, 0.0)
    return lower + upper


def pack_columns(velocity, parts):
    comps, planes, rows_here, span = velocity.shape
    share = span // parts

    def kernel(v_ref, o_ref):
        for d in range(parts):
            pieces = [
                v_ref[c, x, :, share * d : share * (d + 1)] for c in range(comps) for x in range(planes)
            ]
            o_ref[d] = jnp.concatenate(pieces, axis=1)

    return pl.pallas_call(
        kernel,
        out_shape=jax.ShapeDtypeStruct((parts, rows_here, comps * planes * share), jnp.float32),
    )(velocity)


def wall_block(cols, wall_first, wall_second, planes):
    rows, width = cols.shape
    comps = 3
    block = width // comps

    def kernel(c_ref, f_ref, s_ref, o_ref):
        field = c_ref[...]
        first = jnp.dot(f_ref[...], field, precision=HIGHEST, preferred_element_type=jnp.float32)
        second = jnp.dot(s_ref[...], field, precision=HIGHEST, preferred_element_type=jnp.float32)
        v1 = c_ref[:, block : 2 * block]
        for c in range(comps):
            part = slice(c * block, (c + 1) * block)
            o_ref[:, part] = -(v1 * first[:, part]) + viscosity * second[:, part]

    return pl.pallas_call(kernel, out_shape=jax.ShapeDtypeStruct((rows, width), jnp.float32))(
        cols, wall_first, wall_second
    )


def add_ghost(wall, cols, inflow, inlet, planes):
    rows, width = cols.shape
    comps = 3
    share = width // (comps * planes)
    block = planes * share
    lower, upper = ghost_weights(planes)
    gain = np.tile(np.repeat(lower, share), comps)[None, :]
    bias = np.tile(np.repeat(viscosity * upper, share), comps)[None, :]

    def kernel(inlet_ref, w_ref, c_ref, f_ref, g_ref, b_ref, o_ref):
        at_inlet = inlet_ref[0] > 0

        @pl.when(at_inlet)
        def _():
            flow = jnp.concatenate(
                [f_ref[:, c * share : (c + 1) * share] for c in range(comps) for x in range(planes)],
                axis=1,
            )
            first = c_ref[:, 0:block]
            spread = jnp.concatenate([first] * comps, axis=1)
            o_ref[...] = w_ref[...] + flow * (spread * g_ref[...] + b_ref[...])

        @pl.when(jnp.logical_not(at_inlet))
        def _():
            o_ref[...] = w_ref[...]

    vmem = pl.BlockSpec(memory_space=pltpu.VMEM)
    return pl.pallas_call(
        kernel,
        out_shape=jax.ShapeDtypeStruct((rows, width), jnp.float32),
        in_specs=[pl.BlockSpec(memory_space=pltpu.SMEM), vmem, pl.BlockSpec((rows, 256), lambda i: (0, 0))]
        + [vmem] * 3,
        grid=(1,),
        input_output_aliases={1: 0},
    )(inlet, wall, cols, inflow, jnp.asarray(gain, jnp.float32), jnp.asarray(bias, jnp.float32))


def combine(velocity, accumulated, local_terms, back):
    comps, planes, rows_here, span = velocity.shape
    parts = back.shape[0]
    share = span // parts

    partial = keep_rate * accumulated + step_size * local_terms

    def kernel(v_ref, p_ref, b_ref, nv_ref, na_ref):
        for c in range(comps):
            for x in range(planes):
                k = (c * planes + x) * share
                wall = jnp.concatenate([b_ref[d, :, k : k + share] for d in range(parts)], axis=1)
                acc = p_ref[c, x] + step_size * wall
                na_ref[c, x] = acc
                nv_ref[c, x] = v_ref[c, x] + update_rate * acc

    shape = jax.ShapeDtypeStruct(velocity.shape, jnp.float32)
    return pl.pallas_call(kernel, out_shape=(shape, shape))(velocity, partial, back)


def shards(
    velocity, accumulated, wall_first, wall_second, recycle_rows, weight_index, weight_table
):
    comps, planes, rows_here, span = velocity.shape
    parts = lax.axis_size("ga")
    share = span // parts
    rows = rows_here * parts
    width = comps * planes * share

    send = pack_columns(velocity, parts)
    cols = lax.all_to_all(send, "ga", 0, 0, tiled=True).reshape(rows, width)
    mix = interpolation_matrix(recycle_rows, weight_index, weight_table, rows)
    mix, halo_source = lax.optimization_barrier((mix, velocity))
    behind, ahead = halo_planes(halo_source)
    cols, mix, span_source = lax.optimization_barrier((cols, mix, velocity))

    source_slab, source_plane = divmod(RECYCLE_PLANE, planes)
    plane = jnp.concatenate(
        [cols[:, (c * planes + source_plane) * share : (c * planes + source_plane + 1) * share] for c in range(comps)],
        axis=1,
    )
    inflow = jnp.dot(mix, plane, precision=lax.Precision.HIGH, preferred_element_type=jnp.float32)
    inflow = lax.ppermute(inflow, "gx", [(source_slab, 0)])

    wall = wall_block(cols, wall_first, wall_second, planes)
    lines = span_source.reshape(-1, span)
    spectral = jnp.dot(
        lines,
        jnp.asarray(spanwise_table(span)),
        precision=lax.Precision.HIGH,
        preferred_element_type=jnp.float32,
    )
    span_first = spectral[:, :span].reshape(velocity.shape)
    span_second = spectral[:, span:].reshape(velocity.shape)
    span_terms = -(span_source[2:3] * span_first) + viscosity * span_second
    inflow, wall, span_terms = lax.optimization_barrier((inflow, wall, span_terms))

    inlet = (lax.axis_index("gx") == 0).astype(jnp.int32).reshape(1)
    wall = add_ghost(wall, cols, inflow, inlet, planes)
    back = lax.all_to_all(wall.reshape(parts, rows_here, width), "ga", 0, 0, tiled=True)

    local_terms = span_terms + streamwise(velocity, behind, ahead)
    return combine(velocity, accumulated, local_terms, back)


def solution(mesh):
    in_specs = (P(None, "gx", "ga", None), P(None, "gx", "ga", None), P(), P(), P(), P(), P())
    out_specs = (P(None, "gx", "ga", None), P(None, "gx", "ga", None))
    return jax.shard_map(shards, mesh=mesh, in_specs=in_specs, out_specs=out_specs, check_vma=False)
```
